128 devices in a mesh: src: 8 (over z, core), dst: 16 (over x, y).
Axes of the slice: x: 4, y: 4, z: 4, core: 2. Of those that a mesh axis runs over, the one named last changes fastest.
Arguments:
- slab_blocks: bfloat16 [1536, 64, 4096], P(('src', 'dst')), may hold values from -6 to 6
- owner_column: int32 [1536, 1], P(('src', 'dst')), may hold values from 0 to 15; in each aligned block of 12 rows (0 to 11, 12 to 23, ...) at most 3 rows name the same one
- block_row: int32 [1536], P(('src', 'dst')), may hold values from 0 to 3
- block_col: int32 [1536], P(('src', 'dst')), may hold values from 0 to 63
- factor_dst: bfloat16 [65536, 256], P('dst'), may hold values from -0.015136719 to 0.04248047
- factor_slab: bfloat16 [64, 256], replicated, may hold values from -0.0625 to 0.125
- factor_old: float32 [2048, 256], P(('src', 'dst')), may hold values from -6 to 6
Outputs:
- factor_new: float32 [2048, 256], P(('src', 'dst'))
The draws below stay inside these ranges and needn't reach their ends.
Inputs may be any that keep to these rules, and one draw needn't show every extreme that they name: `owner_column`: among one device's 12 blocks, at most 3 name the same owner, a bound that some block reaches.
All inputs are finite; a program needn't handle non-finite values.
Results may differ from the reference program's by a relative error of at most 0.0024.
Values may be sent and summed in bfloat16 or wider, within the bound.
No kernel may reach another device: no remote copies, remote signals or barrier semaphores. Data moves between devices by JAX's collectives and lax.ppermute only.
A program may use at most 192 MiB of HBM per device.

```python
import math
import jax
import jax.numpy as jnp
import numpy as np
from jax import lax

BS = 64
R = 256
IB_DEV = 4
JB_DEV = 64
NB_IN = 12
CAP = 3
NI = 2048
NJ = 65536
BLOCKS = 1536
N_SRC = 8
N_DST = 16


def draw_factor_dst(key, part):
    key_rows, key_values = jax.random.split(key, 2)
    position = jnp.arange(NJ, dtype=jnp.float32)[:, None] / NJ
    scales = jnp.exp(jax.random.uniform(key_rows, (NJ, 1), jnp.float32, jnp.log(0.4), jnp.log(4.0)))
    values = jax.random.uniform(key_values, (NJ, R), jnp.float32, -0.5, 1.0)
    ramp = jnp.exp(jnp.log(3.0) * position)
    factor = 5.0
    norming = factor / jnp.sqrt(jnp.float32(NJ * BS))
    return (values * scales * ramp * norming).astype(jnp.bfloat16)


def touch_ends(result, rng, low, largest):
    extent = result.shape
    index_at = [jax.random.randint(jax.random.fold_in(rng, axis), (), 0, extent[axis]) for axis in range(len(extent))]
    result = result.at[tuple(index_at)].set(low)
    longest = extent.index(max(extent))
    index_at[longest] = (index_at[longest] + 1) % extent[longest]
    return result.at[tuple(index_at)].set(largest)


def shard_levels(own_key, dims, shards, smallest, top_value):
    loudness = 1.0
    for dim, parts in shards:
        heights = jax.random.uniform(jax.random.fold_in(jax.random.fold_in(own_key, 6), dim), (parts,), jnp.float32, smallest / len(shards), top_value / len(shards))
        loudness = loudness * jnp.repeat(jnp.exp(heights), dims[dim] // parts).reshape((-1,) + (1,) * (len(dims) - 1 - dim))
    return loudness


def deal_out(stream_key, own, number, rows, amount, top, most, lean):
    sequence = jax.random.permutation(stream_key, amount)
    crowded, usual = portions_of(amount, rows * top, most, lean, True), portions_of(amount, rows * top, most, lean, False)
    places = jnp.arange(amount)

    def named(tallies, turn):
        used = int((tallies > 0).sum())
        fixed = max(1, used // 4)
        shifted = fixed + (places - fixed + turn * (used - fixed)) % max(1, amount - fixed)
        return jnp.zeros((amount,), jnp.int32).at[sequence[jnp.where(places < fixed, places, shifted)]].set(jnp.asarray(tallies, jnp.int32))

    tallies = jnp.where(number % 4 == 0, named(crowded, number // 4), named(usual, number - number // 4 - 1))
    mixed = jax.random.permutation(jax.random.fold_in(own, 3), amount)
    source_of, taker = mixed[0:amount // 2 * 2:2], mixed[1:amount // 2 * 2:2]
    margin = jnp.minimum(tallies[source_of] - 1, most - tallies[taker]) // 2
    margin = jnp.where((source_of == sequence[0]) | (taker == sequence[0]) | (tallies[taker] == 0), 0, jnp.maximum(margin, 0))
    shifted = jax.random.randint(jax.random.fold_in(own, 4), (amount // 2,), 0, 1 << 20) % (margin + 1)
    tallies = tallies.at[source_of].add(-shifted).at[taker].add(shifted)
    labels = jnp.searchsorted(jnp.cumsum(tallies), jnp.arange(rows * top), side="right").astype(jnp.int32)
    listing = labels.reshape(top, rows).T
    listing = listing[jax.random.permutation(jax.random.fold_in(own, 1), rows)]
    turn = jax.random.randint(jax.random.fold_in(own, 2), (rows, 1), 0, top)
    return jnp.take_along_axis(listing, (jnp.arange(top)[None, :] + turn) % top, axis=1)


def portions_of(count, total, limit, skew, full):
    loads = [(1 << 20) // math.isqrt(grade ** skew) + 1 for grade in range(1, count + 1)]
    largest = limit if full else min(limit, max(-(-total // count), total * loads[0] // sum(loads)))
    least = 1 if total - largest >= count - 1 else 0
    given, rest = [largest] + [least] * (count - 1), total - largest - least * (count - 1)
    while rest > 0:
        free = [i for i in range(1, count) if given[i] < largest] or [i for i in range(1, count) if given[i] < limit]
        mass, budget = sum([loads[i] for i in free]), rest
        for i in free:
            extra = min(limit - given[i], max(1, budget * loads[i] // mass), rest)
            given[i] = given[i] + extra
            rest = rest - extra
    return np.array(given)


def normal_values(key, extent, scale, most, shards=(), held_as=jnp.bfloat16):
    array = jax.random.normal(key, extent, jnp.float32) * scale
    if len(shards) > 0:
        array = shard_levels(key, extent, shards, -0.22, 0.18) * array
    return jnp.clip(array, min=-most, max=most).astype(held_as)


def setup_inputs(seed: int = 0) -> dict:
    streams_of = jax.random.split(jax.random.key(seed), 8)
    slab_blocks = normal_values(streams_of[0], (BLOCKS, BS, BS * BS), 1.0, 6.0, ((0, 128),))
    owner_column_keys = jax.random.split(jax.random.fold_in(streams_of[1], 1), BLOCKS // NB_IN)
    owner_column_turns = jax.random.permutation(jax.random.fold_in(streams_of[1], 3), BLOCKS // NB_IN)
    owner_column = jax.vmap(lambda own, number: deal_out(jax.random.fold_in(streams_of[1], 2), own, number, NB_IN, N_DST, 1, CAP, 2))(owner_column_keys, owner_column_turns).reshape((BLOCKS, 1))
    block_row = touch_ends(jax.random.randint(streams_of[2], (BLOCKS,), 0, IB_DEV), jax.random.fold_in(streams_of[2], 1), 0, IB_DEV - 1).astype(jnp.int32)
    block_col = touch_ends(jax.random.randint(streams_of[3], (BLOCKS,), 0, JB_DEV), jax.random.fold_in(streams_of[3], 1), 0, JB_DEV - 1).astype(jnp.int32)
    factor_dst = draw_factor_dst(jax.random.fold_in(streams_of[7], 71), 0)
    factor_slab = jnp.clip(jax.random.uniform(streams_of[5], (BS, R), jnp.float32, -0.0625, 0.125), -0.0625, 0.125).astype(jnp.bfloat16)
    factor_old = normal_values(streams_of[6], (NI, R), 1.0, 6.0, ((0, 128),), jnp.float32)
    return dict(slab_blocks=slab_blocks, owner_column=owner_column, block_row=block_row, block_col=block_col, factor_dst=factor_dst, factor_slab=factor_slab, factor_old=factor_old)


def reference(slab_blocks, owner_column, block_row, block_col, factor_dst, factor_slab, factor_old):
    count = slab_blocks.shape[0]
    per_src = count // N_SRC
    order = jnp.arange(count, dtype=jnp.int32)
    row_block = (order // per_src).astype(jnp.int32) * IB_DEV + block_row.astype(jnp.int32)
    col_block = owner_column[:, 0].astype(jnp.int32) * JB_DEV + block_col.astype(jnp.int32)
    tiles = factor_dst.reshape(NJ // BS, BS, R)
    slab = factor_slab.astype(jnp.float32)

    def one_block(item):
        block, column = item
        left = tiles[column].astype(jnp.float32)
        khatri = (left[:, None, :] * slab[None, :, :]).reshape(BS * BS, R).astype(jnp.bfloat16)
        khatri = lax.optimization_barrier(khatri).astype(jnp.float32)
        return jnp.dot(block.astype(jnp.float32), khatri, precision=lax.Precision.HIGHEST)
    results = lax.map(one_block, (slab_blocks, col_block))
    summed = jax.ops.segment_sum(results, row_block, num_segments=NI // BS)
    mttkrp = summed.reshape(NI, R)
    gram_left = jnp.dot(factor_dst.T.astype(jnp.float32), factor_dst.astype(jnp.float32), preferred_element_type=jnp.float32)
    gram_right = jnp.dot(factor_slab.T.astype(jnp.float32), factor_slab.astype(jnp.float32), preferred_element_type=jnp.float32)
    gram = gram_left * gram_right + 0.1 * jnp.eye(R, dtype=jnp.float32)
    lower = jnp.linalg.cholesky(gram)
    target = mttkrp + 0.1 * factor_old
    return jax.scipy.linalg.cho_solve((lower, True), target.T).T
```

```python
import functools

import jax
import jax.numpy as jnp
from jax import lax
from jax.experimental import pallas as pl
from jax.experimental.pallas import tpu as pltpu
from jax.sharding import PartitionSpec as P

RIDGE = 0.1


def mttkrp_kernel(rows_ref, places_ref, x_ref, left_ref, slab_ref, out_ref, kr_ref):
    step = pl.program_id(0)

    @pl.when(step == 0)
    def _():
        out_ref[...] = jnp.zeros_like(out_ref)

    left = left_ref[0].astype(jnp.float32)
    slab = slab_ref[...].astype(jnp.float32)
    edge = left.shape[0]
    bins = slab.shape[0]
    for b in range(edge):
        kr_ref[pl.ds(b * bins, bins), :] = (left[b : b + 1, :] * slab).astype(kr_ref.dtype)
    prod = jnp.dot(x_ref[0], kr_ref[...], preferred_element_type=jnp.float32)
    row = rows_ref[step]
    out_ref[row] = out_ref[row] + prod


def block_products(slab_blocks, received, places, block_row, factor_slab, row_blocks):
    count, edge, depth_k = slab_blocks.shape
    width = received.shape[2]
    grid_spec = pltpu.PrefetchScalarGridSpec(
        num_scalar_prefetch=2,
        grid=(count,),
        in_specs=[
            pl.BlockSpec((1, edge, depth_k), lambda i, rows, pl_: (i, 0, 0)),
            pl.BlockSpec((1, received.shape[1], width), lambda i, rows, pl_: (pl_[i], 0, 0)),
            pl.BlockSpec(factor_slab.shape, lambda i, rows, pl_: (0, 0)),
        ],
        out_specs=pl.BlockSpec((row_blocks, edge, width), lambda i, rows, pl_: (0, 0, 0)),
        scratch_shapes=[pltpu.VMEM((depth_k, width), jnp.bfloat16)],
    )
    flops = 2 * count * edge * depth_k * width
    return pl.pallas_call(
        mttkrp_kernel,
        grid_spec=grid_spec,
        out_shape=jax.ShapeDtypeStruct((row_blocks, edge, width), jnp.float32),
        compiler_params=pltpu.CompilerParams(
            dimension_semantics=("arbitrary",), vmem_limit_bytes=48 * 1024 * 1024
        ),
        cost_estimate=pl.CostEstimate(
            flops=flops,
            bytes_accessed=slab_blocks.size * 2 + count * edge * width * 2 + row_blocks * edge * width * 4,
            transcendentals=0,
        ),
    )(block_row, places, slab_blocks, received, factor_slab)


def shards(slab_blocks, owner_column, block_row, block_col, factor_dst, factor_slab, factor_old):
    peers = lax.axis_size("dst")
    count = slab_blocks.shape[0]
    edge = slab_blocks.shape[1]
    width = factor_dst.shape[1]
    depth = max(2, 4 * count // peers)
    owners = owner_column[:, 0]
    order = jnp.arange(count, dtype=jnp.int32)
    same = (owners[:, None] == owners[None, :]) & (order[None, :] < order[:, None])
    places = owners * depth + jnp.sum(same.astype(jnp.int32), axis=1)
    slot_ids = jnp.arange(peers * depth, dtype=jnp.int32)
    match = places[None, :] == slot_ids[:, None]
    requests = jnp.sum(jnp.where(match, block_col[None, :], 0), axis=1).reshape(peers, depth)
    asked = lax.all_to_all(requests, "dst", split_axis=0, concat_axis=0, tiled=True)
    tiles_dst = factor_dst.reshape(factor_dst.shape[0] // edge, edge, width)
    outgoing = tiles_dst[asked.reshape(peers * depth)].reshape(peers, depth, edge, width)
    received = lax.all_to_all(outgoing, "dst", split_axis=0, concat_axis=0, tiled=True)
    received = received.reshape(peers * depth, edge, width)

    row_blocks = factor_old.shape[0] * peers // edge
    partial_sum = block_products(slab_blocks, received, places, block_row, factor_slab, row_blocks)
    partial_sum = partial_sum.reshape(row_blocks * edge, width)
    summed_rows = lax.psum_scatter(partial_sum, "dst", scatter_dimension=0, tiled=True)

    local_gram = jnp.dot(factor_dst.T, factor_dst, preferred_element_type=jnp.float32)
    gram_left = lax.psum(local_gram, "dst")
    gram_right = jnp.dot(factor_slab.T, factor_slab, preferred_element_type=jnp.float32)
    gram = gram_left * gram_right + RIDGE * jnp.eye(width, dtype=jnp.float32)
    lower = jnp.linalg.cholesky(gram)
    target = summed_rows + RIDGE * factor_old
    return jax.scipy.linalg.cho_solve((lower, True), target.T).T


def solution(mesh):
    placed = (
        P(("src", "dst"), None, None),
        P(("src", "dst"), None),
        P(("src", "dst")),
        P(("src", "dst")),
        P("dst", None),
        P(),
        P(("src", "dst"), None),
    )
    return jax.shard_map(
        shards, mesh=mesh, in_specs=placed, out_specs=P(("src", "dst"), None), check_vma=False
    )
```

```python
import functools

import jax
import jax.numpy as jnp
from jax import lax
from jax.experimental import pallas as pl
from jax.experimental.pallas import tpu as pltpu
from jax.sharding import PartitionSpec as P

RIDGE = 0.1


def mttkrp_kernel(rows_ref, places_ref, x_ref, left_ref, slab_ref, out_ref, kr_ref):
    step = pl.program_id(0)

    @pl.when(step == 0)
    def _():
        out_ref[...] = jnp.zeros_like(out_ref)

    left = left_ref[0].astype(jnp.float32)
    slab = slab_ref[...].astype(jnp.float32)
    edge = left.shape[0]
    bins = slab.shape[0]
    for b in range(edge):
        kr_ref[pl.ds(b * bins, bins), :] = (left[b : b + 1, :] * slab).astype(kr_ref.dtype)
    prod = jnp.dot(x_ref[0], kr_ref[...], preferred_element_type=jnp.float32)
    row = rows_ref[step]
    out_ref[row] = out_ref[row] + prod


def block_products(slab_blocks, received, places, block_row, factor_slab, row_blocks):
    count, edge, depth_k = slab_blocks.shape
    width = received.shape[2]
    grid_spec = pltpu.PrefetchScalarGridSpec(
        num_scalar_prefetch=2,
        grid=(count,),
        in_specs=[
            pl.BlockSpec((1, edge, depth_k), lambda i, rows, pl_: (i, 0, 0)),
            pl.BlockSpec((1, received.shape[1], width), lambda i, rows, pl_: (pl_[i], 0, 0)),
            pl.BlockSpec(factor_slab.shape, lambda i, rows, pl_: (0, 0)),
        ],
        out_specs=pl.BlockSpec((row_blocks, edge, width), lambda i, rows, pl_: (0, 0, 0)),
        scratch_shapes=[pltpu.VMEM((depth_k, width), jnp.bfloat16)],
    )
    flops = 2 * count * edge * depth_k * width
    return pl.pallas_call(
        mttkrp_kernel,
        grid_spec=grid_spec,
        out_shape=jax.ShapeDtypeStruct((row_blocks, edge, width), jnp.float32),
        compiler_params=pltpu.CompilerParams(
            dimension_semantics=("arbitrary",), vmem_limit_bytes=48 * 1024 * 1024
        ),
        cost_estimate=pl.CostEstimate(
            flops=flops,
            bytes_accessed=slab_blocks.size * 2 + count * edge * width * 2 + row_blocks * edge * width * 4,
            transcendentals=0,
        ),
    )(block_row, places, slab_blocks, received, factor_slab)


def scatter_sum(rows, peers):
    pieces = rows.reshape(peers, rows.shape[0] // peers, rows.shape[1])
    arrived = lax.all_to_all(pieces, "dst", split_axis=0, concat_axis=0, tiled=True)
    return jnp.sum(arrived, axis=0)


def shards(slab_blocks, owner_column, block_row, block_col, factor_dst, factor_slab, factor_old):
    peers = lax.axis_size("dst")
    count = slab_blocks.shape[0]
    edge = slab_blocks.shape[1]
    width = factor_dst.shape[1]
    depth = max(2, 4 * count // peers)
    owners = owner_column[:, 0]
    order = jnp.arange(count, dtype=jnp.int32)
    same = (owners[:, None] == owners[None, :]) & (order[None, :] < order[:, None])
    places = owners * depth + jnp.sum(same.astype(jnp.int32), axis=1)
    slot_ids = jnp.arange(peers * depth, dtype=jnp.int32)
    match = places[None, :] == slot_ids[:, None]
    requests = jnp.sum(jnp.where(match, block_col[None, :], 0), axis=1).reshape(peers, depth)
    asked = lax.all_to_all(requests, "dst", split_axis=0, concat_axis=0, tiled=True)
    tiles_dst = factor_dst.reshape(factor_dst.shape[0] // edge, edge, width)
    outgoing = tiles_dst[asked.reshape(peers * depth)].reshape(peers, depth, edge, width)
    received = lax.all_to_all(outgoing, "dst", split_axis=0, concat_axis=0, tiled=True)
    received = received.reshape(peers * depth, edge, width)

    row_blocks = factor_old.shape[0] * peers // edge
    partial_sum = block_products(slab_blocks, received, places, block_row, factor_slab, row_blocks)
    partial_sum = partial_sum.reshape(row_blocks * edge, width)
    summed_rows = scatter_sum(partial_sum, peers)

    local_gram = jnp.dot(factor_dst.T, factor_dst, preferred_element_type=jnp.float32)
    gram_rows = scatter_sum(local_gram, peers)
    gram_left = lax.all_gather(gram_rows, "dst", axis=0, tiled=True)
    gram_right = jnp.dot(factor_slab.T, factor_slab, preferred_element_type=jnp.float32)
    gram = gram_left * gram_right + RIDGE * jnp.eye(width, dtype=jnp.float32)
    lower = jnp.linalg.cholesky(gram)
    target = summed_rows + RIDGE * factor_old
    return jax.scipy.linalg.cho_solve((lower, True), target.T).T


def solution(mesh):
    placed = (
        P(("src", "dst"), None, None),
        P(("src", "dst"), None),
        P(("src", "dst")),
        P(("src", "dst")),
        P("dst", None),
        P(),
        P(("src", "dst"), None),
    )
    return jax.shard_map(
        shards, mesh=mesh, in_specs=placed, out_specs=P(("src", "dst"), None), check_vma=False
    )
```

```python
import functools

import jax
import jax.numpy as jnp
from jax import lax
from jax.experimental import pallas as pl
from jax.experimental.pallas import tpu as pltpu
from jax.sharding import PartitionSpec as P

RIDGE = 0.1


def mttkrp_kernel(rows_ref, places_ref, x_ref, left_ref, slab_ref, out_ref, kr_ref):
    step = pl.program_id(0)

    @pl.when(step == 0)
    def _():
        out_ref[...] = jnp.zeros_like(out_ref)

    left = left_ref[0].astype(jnp.float32)
    slab = slab_ref[...].astype(jnp.float32)
    edge = left.shape[0]
    bins = slab.shape[0]
    for b in range(edge):
        kr_ref[pl.ds(b * bins, bins), :] = (left[b : b + 1, :] * slab).astype(kr_ref.dtype)
    prod = jnp.dot(x_ref[0], kr_ref[...], preferred_element_type=jnp.float32)
    row = rows_ref[step]
    out_ref[row] = out_ref[row] + prod


def block_products(slab_blocks, received, places, block_row, factor_slab, row_blocks):
    count, edge, depth_k = slab_blocks.shape
    width = received.shape[2]
    grid_spec = pltpu.PrefetchScalarGridSpec(
        num_scalar_prefetch=2,
        grid=(count,),
        in_specs=[
            pl.BlockSpec((1, edge, depth_k), lambda i, rows, pl_: (i, 0, 0)),
            pl.BlockSpec((1, received.shape[1], width), lambda i, rows, pl_: (pl_[i], 0, 0)),
            pl.BlockSpec(factor_slab.shape, lambda i, rows, pl_: (0, 0)),
        ],
        out_specs=pl.BlockSpec((row_blocks, edge, width), lambda i, rows, pl_: (0, 0, 0)),
        scratch_shapes=[pltpu.VMEM((depth_k, width), jnp.bfloat16)],
    )
    flops = 2 * count * edge * depth_k * width
    return pl.pallas_call(
        mttkrp_kernel,
        grid_spec=grid_spec,
        out_shape=jax.ShapeDtypeStruct((row_blocks, edge, width), jnp.float32),
        compiler_params=pltpu.CompilerParams(
            dimension_semantics=("arbitrary",), vmem_limit_bytes=48 * 1024 * 1024
        ),
        cost_estimate=pl.CostEstimate(
            flops=flops,
            bytes_accessed=slab_blocks.size * 2 + count * edge * width * 2 + row_blocks * edge * width * 4,
            transcendentals=0,
        ),
    )(block_row, places, slab_blocks, received, factor_slab)


def scatter_sum(rows, peers):
    pieces = rows.reshape(peers, rows.shape[0] // peers, rows.shape[1])
    arrived = lax.all_to_all(pieces, "dst", split_axis=0, concat_axis=0, tiled=True)
    return jnp.sum(arrived, axis=0)


def shards(slab_blocks, owner_column, block_row, block_col, factor_dst, factor_slab, factor_old):
    peers = lax.axis_size("dst")
    count = slab_blocks.shape[0]
    edge = slab_blocks.shape[1]
    width = factor_dst.shape[1]
    depth = max(2, 4 * count // peers)
    owners = owner_column[:, 0]
    order = jnp.arange(count, dtype=jnp.int32)
    same = (owners[:, None] == owners[None, :]) & (order[None, :] < order[:, None])
    places = owners * depth + jnp.sum(same.astype(jnp.int32), axis=1)
    slot_ids = jnp.arange(peers * depth, dtype=jnp.int32)
    match = places[None, :] == slot_ids[:, None]
    requests = jnp.sum(jnp.where(match, block_col[None, :], 0), axis=1).reshape(peers, depth)
    local_gram = jnp.dot(factor_dst.T, factor_dst, preferred_element_type=jnp.float32)
    chunk = local_gram.shape[0] // peers
    asked_row = jnp.zeros((peers, 1, width), jnp.float32).at[:, 0, :depth].set(requests.astype(jnp.float32))
    first = jnp.concatenate([local_gram.reshape(peers, chunk, width), asked_row], axis=1)
    first = lax.all_to_all(first, "dst", split_axis=0, concat_axis=0, tiled=True)
    gram_rows = jnp.sum(first[:, :chunk, :], axis=0)
    asked = first[:, chunk, :depth].astype(jnp.int32)
    spread = jnp.broadcast_to(gram_rows[None], (peers, chunk, width))
    gram_left = lax.all_to_all(spread, "dst", split_axis=0, concat_axis=0, tiled=True)
    gram_left = gram_left.reshape(peers * chunk, width)
    tiles_dst = factor_dst.reshape(factor_dst.shape[0] // edge, edge, width)
    outgoing = tiles_dst[asked.reshape(peers * depth)].reshape(peers, depth, edge, width)
    received = lax.all_to_all(outgoing, "dst", split_axis=0, concat_axis=0, tiled=True)
    received = received.reshape(peers * depth, edge, width)

    row_blocks = factor_old.shape[0] * peers // edge
    partial_sum = block_products(slab_blocks, received, places, block_row, factor_slab, row_blocks)
    partial_sum = partial_sum.reshape(row_blocks * edge, width)
    summed_rows = scatter_sum(partial_sum, peers)

    gram_right = jnp.dot(factor_slab.T, factor_slab, preferred_element_type=jnp.float32)
    gram = gram_left * gram_right + RIDGE * jnp.eye(width, dtype=jnp.float32)
    lower = jnp.linalg.cholesky(gram)
    target = summed_rows + RIDGE * factor_old
    return jax.scipy.linalg.cho_solve((lower, True), target.T).T


def solution(mesh):
    placed = (
        P(("src", "dst"), None, None),
        P(("src", "dst"), None),
        P(("src", "dst")),
        P(("src", "dst")),
        P("dst", None),
        P(),
        P(("src", "dst"), None),
    )
    return jax.shard_map(
        shards, mesh=mesh, in_specs=placed, out_specs=P(("src", "dst"), None), check_vma=False
    )
```

```python
import functools

import jax
import jax.numpy as jnp
from jax import lax
from jax.experimental import pallas as pl
from jax.experimental.pallas import tpu as pltpu
from jax.sharding import PartitionSpec as P

RIDGE = 0.1


def mttkrp_kernel(rows_ref, places_ref, x_ref, left_ref, slab_ref, out_ref, kr_ref):
    step = pl.program_id(0)

    @pl.when(step == 0)
    def _():
        out_ref[...] = jnp.zeros_like(out_ref)

    left = left_ref[0].astype(jnp.float32)
    slab = slab_ref[...].astype(jnp.float32)
    edge = left.shape[0]
    bins = slab.shape[0]
    for b in range(edge):
        kr_ref[pl.ds(b * bins, bins), :] = (left[b : b + 1, :] * slab).astype(kr_ref.dtype)
    prod = jnp.dot(x_ref[0], kr_ref[...], preferred_element_type=jnp.float32)
    row = rows_ref[step]
    out_ref[row] = out_ref[row] + prod


def block_products(slab_blocks, received, places, block_row, factor_slab, row_blocks):
    count, edge, depth_k = slab_blocks.shape
    width = received.shape[2]
    grid_spec = pltpu.PrefetchScalarGridSpec(
        num_scalar_prefetch=2,
        grid=(count,),
        in_specs=[
            pl.BlockSpec((1, edge, depth_k), lambda i, rows, pl_: (i, 0, 0)),
            pl.BlockSpec((1, received.shape[1], width), lambda i, rows, pl_: (pl_[i], 0, 0)),
            pl.BlockSpec(factor_slab.shape, lambda i, rows, pl_: (0, 0)),
        ],
        out_specs=pl.BlockSpec((row_blocks, edge, width), lambda i, rows, pl_: (0, 0, 0)),
        scratch_shapes=[pltpu.VMEM((depth_k, width), jnp.bfloat16)],
    )
    flops = 2 * count * edge * depth_k * width
    return pl.pallas_call(
        mttkrp_kernel,
        grid_spec=grid_spec,
        out_shape=jax.ShapeDtypeStruct((row_blocks, edge, width), jnp.float32),
        compiler_params=pltpu.CompilerParams(
            dimension_semantics=("arbitrary",), vmem_limit_bytes=48 * 1024 * 1024
        ),
        cost_estimate=pl.CostEstimate(
            flops=flops,
            bytes_accessed=slab_blocks.size * 2 + count * edge * width * 2 + row_blocks * edge * width * 4,
            transcendentals=0,
        ),
    )(block_row, places, slab_blocks, received, factor_slab)


def scatter_sum(rows, peers):
    pieces = rows.reshape(peers, rows.shape[0] // peers, rows.shape[1])
    arrived = lax.all_to_all(pieces, "dst", split_axis=0, concat_axis=0, tiled=True)
    return jnp.sum(arrived, axis=0)


def ridge_inverse(gram):
    eye = jnp.eye(gram.shape[0], dtype=jnp.float32)
    start = eye / jnp.max(jnp.sum(jnp.abs(gram), axis=1))

    def going(state):
        steps, _, norm = state
        return (norm >= 1e-3) & (steps < 64)

    def step(state):
        steps, inverse, _ = state
        residual = eye - jnp.dot(gram, inverse, precision=lax.Precision.HIGHEST)
        norm = jnp.max(jnp.sum(jnp.abs(residual), axis=1))
        inverse = inverse + jnp.dot(inverse, residual, precision=lax.Precision.HIGHEST)
        return steps + 1, inverse, norm

    _, inverse, _ = lax.while_loop(going, step, (jnp.int32(0), start, jnp.float32(2.0)))
    return inverse


def shards(slab_blocks, owner_column, block_row, block_col, factor_dst, factor_slab, factor_old):
    peers = lax.axis_size("dst")
    count = slab_blocks.shape[0]
    edge = slab_blocks.shape[1]
    width = factor_dst.shape[1]
    depth = max(2, 4 * count // peers)
    owners = owner_column[:, 0]
    order = jnp.arange(count, dtype=jnp.int32)
    same = (owners[:, None] == owners[None, :]) & (order[None, :] < order[:, None])
    places = owners * depth + jnp.sum(same.astype(jnp.int32), axis=1)
    slot_ids = jnp.arange(peers * depth, dtype=jnp.int32)
    match = places[None, :] == slot_ids[:, None]
    requests = jnp.sum(jnp.where(match, block_col[None, :], 0), axis=1).reshape(peers, depth)
    local_gram = jnp.dot(factor_dst.T, factor_dst, preferred_element_type=jnp.float32)
    chunk = local_gram.shape[0] // peers
    asked_row = jnp.zeros((peers, 1, width), jnp.float32).at[:, 0, :depth].set(requests.astype(jnp.float32))
    first = jnp.concatenate([local_gram.reshape(peers, chunk, width), asked_row], axis=1)
    first = lax.all_to_all(first, "dst", split_axis=0, concat_axis=0, tiled=True)
    gram_rows = jnp.sum(first[:, :chunk, :], axis=0)
    asked = first[:, chunk, :depth].astype(jnp.int32)
    spread = jnp.broadcast_to(gram_rows[None], (peers, chunk, width))
    gram_left = lax.all_to_all(spread, "dst", split_axis=0, concat_axis=0, tiled=True)
    gram_left = gram_left.reshape(peers * chunk, width)
    tiles_dst = factor_dst.reshape(factor_dst.shape[0] // edge, edge, width)
    outgoing = tiles_dst[asked.reshape(peers * depth)].reshape(peers, depth, edge, width)
    received = lax.all_to_all(outgoing, "dst", split_axis=0, concat_axis=0, tiled=True)
    received = received.reshape(peers * depth, edge, width)

    row_blocks = factor_old.shape[0] * peers // edge
    partial_sum = block_products(slab_blocks, received, places, block_row, factor_slab, row_blocks)
    partial_sum = partial_sum.reshape(row_blocks * edge, width)
    partial_sum, gram_left = lax.optimization_barrier((partial_sum, gram_left))
    summed_rows = scatter_sum(partial_sum, peers)

    gram_right = jnp.dot(factor_slab.T, factor_slab, preferred_element_type=jnp.float32)
    gram = gram_left * gram_right + RIDGE * jnp.eye(width, dtype=jnp.float32)
    inverse = ridge_inverse(gram)
    target = summed_rows + RIDGE * factor_old
    return jnp.dot(target, inverse, precision=lax.Precision.HIGHEST)


def solution(mesh):
    placed = (
        P(("src", "dst"), None, None),
        P(("src", "dst"), None),
        P(("src", "dst")),
        P(("src", "dst")),
        P("dst", None),
        P(),
        P(("src", "dst"), None),
    )
    return jax.shard_map(
        shards, mesh=mesh, in_specs=placed, out_specs=P(("src", "dst"), None), check_vma=False
    )
```

```python
import functools

import jax
import jax.numpy as jnp
from jax import lax
from jax.experimental import pallas as pl
from jax.experimental.pallas import tpu as pltpu
from jax.sharding import PartitionSpec as P

RIDGE = 0.1


def mttkrp_kernel(rows_ref, places_ref, x_ref, left_ref, slab_ref, out_ref, kr_ref):
    step = pl.program_id(0)

    @pl.when(step == 0)
    def _():
        out_ref[...] = jnp.zeros_like(out_ref)

    left = left_ref[0].astype(jnp.float32)
    slab = slab_ref[...].astype(jnp.float32)
    edge = left.shape[0]
    bins = slab.shape[0]
    for b in range(edge):
        kr_ref[pl.ds(b * bins, bins), :] = (left[b : b + 1, :] * slab).astype(kr_ref.dtype)
    prod = jnp.dot(x_ref[0], kr_ref[...], preferred_element_type=jnp.float32)
    row = rows_ref[step]
    out_ref[row] = out_ref[row] + prod


def block_products(slab_blocks, received, places, block_row, factor_slab, row_blocks):
    count, edge, depth_k = slab_blocks.shape
    width = received.shape[2]
    grid_spec = pltpu.PrefetchScalarGridSpec(
        num_scalar_prefetch=2,
        grid=(count,),
        in_specs=[
            pl.BlockSpec((1, edge, depth_k), lambda i, rows, pl_: (i, 0, 0)),
            pl.BlockSpec((1, received.shape[1], width), lambda i, rows, pl_: (pl_[i], 0, 0)),
            pl.BlockSpec(factor_slab.shape, lambda i, rows, pl_: (0, 0)),
        ],
        out_specs=pl.BlockSpec((row_blocks, edge, width), lambda i, rows, pl_: (0, 0, 0)),
        scratch_shapes=[pltpu.VMEM((depth_k, width), jnp.bfloat16)],
    )
    flops = 2 * count * edge * depth_k * width
    return pl.pallas_call(
        mttkrp_kernel,
        grid_spec=grid_spec,
        out_shape=jax.ShapeDtypeStruct((row_blocks, edge, width), jnp.float32),
        compiler_params=pltpu.CompilerParams(
            dimension_semantics=("arbitrary",), vmem_limit_bytes=48 * 1024 * 1024
        ),
        cost_estimate=pl.CostEstimate(
            flops=flops,
            bytes_accessed=slab_blocks.size * 2 + count * edge * width * 2 + row_blocks * edge * width * 4,
            transcendentals=0,
        ),
    )(block_row, places, slab_blocks, received, factor_slab)


def scatter_sum(rows, peers):
    pieces = rows.reshape(peers, rows.shape[0] // peers, rows.shape[1])
    arrived = lax.all_to_all(pieces, "dst", split_axis=0, concat_axis=0, tiled=True)
    return jnp.sum(arrived, axis=0)


def ridge_inverse(gram):
    eye = jnp.eye(gram.shape[0], dtype=jnp.float32)
    start = eye / jnp.max(jnp.sum(jnp.abs(gram), axis=1))

    def going(state):
        steps, _, norm = state
        return (norm >= 1e-3) & (steps < 64)

    def step(state):
        steps, inverse, _ = state
        residual = eye - jnp.dot(gram, inverse, precision=lax.Precision.HIGHEST)
        norm = jnp.max(jnp.sum(jnp.abs(residual), axis=1))
        inverse = inverse + jnp.dot(inverse, residual, precision=lax.Precision.HIGHEST)
        return steps + 1, inverse, norm

    inverse = start
    for _ in range(9):
        inverse = inverse + jnp.dot(
            inverse, eye - jnp.dot(gram, inverse, precision=lax.Precision.HIGHEST), precision=lax.Precision.HIGHEST
        )
    _, inverse, _ = lax.while_loop(going, step, (jnp.int32(0), inverse, jnp.float32(2.0)))
    return inverse


def shards(slab_blocks, owner_column, block_row, block_col, factor_dst, factor_slab, factor_old):
    peers = lax.axis_size("dst")
    count = slab_blocks.shape[0]
    edge = slab_blocks.shape[1]
    width = factor_dst.shape[1]
    depth = max(2, 4 * count // peers)
    owners = owner_column[:, 0]
    order = jnp.arange(count, dtype=jnp.int32)
    same = (owners[:, None] == owners[None, :]) & (order[None, :] < order[:, None])
    places = owners * depth + jnp.sum(same.astype(jnp.int32), axis=1)
    slot_ids = jnp.arange(peers * depth, dtype=jnp.int32)
    match = places[None, :] == slot_ids[:, None]
    requests = jnp.sum(jnp.where(match, block_col[None, :], 0), axis=1).reshape(peers, depth)
    local_gram = jnp.dot(factor_dst.T, factor_dst, preferred_element_type=jnp.float32)
    chunk = local_gram.shape[0] // peers
    asked_row = jnp.zeros((peers, 1, width), jnp.float32).at[:, 0, :depth].set(requests.astype(jnp.float32))
    first = jnp.concatenate([local_gram.reshape(peers, chunk, width), asked_row], axis=1)
    first = lax.all_to_all(first, "dst", split_axis=0, concat_axis=0, tiled=True)
    gram_rows = jnp.sum(first[:, :chunk, :], axis=0)
    asked = first[:, chunk, :depth].astype(jnp.int32)
    spread = jnp.broadcast_to(gram_rows[None], (peers, chunk, width))
    gram_left = lax.all_to_all(spread, "dst", split_axis=0, concat_axis=0, tiled=True)
    gram_left = gram_left.reshape(peers * chunk, width)
    tiles_dst = factor_dst.reshape(factor_dst.shape[0] // edge, edge, width)
    outgoing = tiles_dst[asked.reshape(peers * depth)].reshape(peers, depth, edge, width)
    received = lax.all_to_all(outgoing, "dst", split_axis=0, concat_axis=0, tiled=True)
    received = received.reshape(peers * depth, edge, width)

    row_blocks = factor_old.shape[0] * peers // edge
    partial_sum = block_products(slab_blocks, received, places, block_row, factor_slab, row_blocks)
    partial_sum = partial_sum.reshape(row_blocks * edge, width)
    partial_sum, gram_left = lax.optimization_barrier((partial_sum, gram_left))
    summed_rows = scatter_sum(partial_sum, peers)

    gram_right = jnp.dot(factor_slab.T, factor_slab, preferred_element_type=jnp.float32)
    gram = gram_left * gram_right + RIDGE * jnp.eye(width, dtype=jnp.float32)
    inverse = ridge_inverse(gram)
    target = summed_rows + RIDGE * factor_old
    return jnp.dot(target, inverse, precision=lax.Precision.HIGHEST)


def solution(mesh):
    placed = (
        P(("src", "dst"), None, None),
        P(("src", "dst"), None),
        P(("src", "dst")),
        P(("src", "dst")),
        P("dst", None),
        P(),
        P(("src", "dst"), None),
    )
    return jax.shard_map(
        shards, mesh=mesh, in_specs=placed, out_specs=P(("src", "dst"), None), check_vma=False
    )
```

```python
import functools

import jax
import jax.numpy as jnp
from jax import lax
from jax.experimental import pallas as pl
from jax.experimental.pallas import tpu as pltpu
from jax.sharding import PartitionSpec as P

RIDGE = 0.1


def mttkrp_kernel(rows_ref, places_ref, x_ref, left_ref, slab_ref, out_ref, kr_ref):
    step = pl.program_id(0)

    @pl.when(step == 0)
    def _():
        out_ref[...] = jnp.zeros_like(out_ref)

    left = left_ref[0]
    slab = slab_ref[...]
    edge = left.shape[0]
    bins = slab.shape[0]
    for b in range(edge):
        kr_ref[pl.ds(b * bins, bins), :] = (left[b : b + 1, :] * slab).astype(kr_ref.dtype)
    prod = jnp.dot(x_ref[0], kr_ref[...], preferred_element_type=jnp.float32)
    row = rows_ref[step]
    out_ref[row] = out_ref[row] + prod


def block_products(slab_blocks, received, places, block_row, factor_slab, row_blocks):
    count, edge, depth_k = slab_blocks.shape
    width = received.shape[2]
    grid_spec = pltpu.PrefetchScalarGridSpec(
        num_scalar_prefetch=2,
        grid=(count,),
        in_specs=[
            pl.BlockSpec((1, edge, depth_k), lambda i, rows, pl_: (i, 0, 0)),
            pl.BlockSpec((1, received.shape[1], width), lambda i, rows, pl_: (pl_[i], 0, 0)),
            pl.BlockSpec(factor_slab.shape, lambda i, rows, pl_: (0, 0)),
        ],
        out_specs=pl.BlockSpec((row_blocks, edge, width), lambda i, rows, pl_: (0, 0, 0)),
        scratch_shapes=[pltpu.VMEM((depth_k, width), jnp.bfloat16)],
    )
    flops = 2 * count * edge * depth_k * width
    return pl.pallas_call(
        mttkrp_kernel,
        grid_spec=grid_spec,
        out_shape=jax.ShapeDtypeStruct((row_blocks, edge, width), jnp.float32),
        compiler_params=pltpu.CompilerParams(
            dimension_semantics=("arbitrary",), vmem_limit_bytes=48 * 1024 * 1024
        ),
        cost_estimate=pl.CostEstimate(
            flops=flops,
            bytes_accessed=slab_blocks.size * 2 + count * edge * width * 2 + row_blocks * edge * width * 4,
            transcendentals=0,
        ),
    )(block_row, places, slab_blocks, received, factor_slab)


def scatter_sum(rows, peers):
    pieces = rows.reshape(peers, rows.shape[0] // peers, rows.shape[1])
    arrived = lax.all_to_all(pieces, "dst", split_axis=0, concat_axis=0, tiled=True)
    return jnp.sum(arrived, axis=0)


def ridge_inverse(gram):
    eye = jnp.eye(gram.shape[0], dtype=jnp.float32)
    start = eye / jnp.max(jnp.sum(jnp.abs(gram), axis=1))

    def going(state):
        steps, _, norm = state
        return (norm >= 1e-3) & (steps < 64)

    def step(state):
        steps, inverse, _ = state
        residual = eye - jnp.dot(gram, inverse, precision=lax.Precision.HIGHEST)
        norm = jnp.max(jnp.sum(jnp.abs(residual), axis=1))
        inverse = inverse + jnp.dot(inverse, residual, precision=lax.Precision.HIGHEST)
        return steps + 1, inverse, norm

    inverse = start
    for _ in range(9):
        inverse = inverse + jnp.dot(
            inverse, eye - jnp.dot(gram, inverse, precision=lax.Precision.HIGHEST), precision=lax.Precision.HIGHEST
        )
    _, inverse, _ = lax.while_loop(going, step, (jnp.int32(0), inverse, jnp.float32(2.0)))
    return inverse


def shards(slab_blocks, owner_column, block_row, block_col, factor_dst, factor_slab, factor_old):
    peers = lax.axis_size("dst")
    count = slab_blocks.shape[0]
    edge = slab_blocks.shape[1]
    width = factor_dst.shape[1]
    depth = max(2, 4 * count // peers)
    owners = owner_column[:, 0]
    order = jnp.arange(count, dtype=jnp.int32)
    same = (owners[:, None] == owners[None, :]) & (order[None, :] < order[:, None])
    places = owners * depth + jnp.sum(same.astype(jnp.int32), axis=1)
    slot_ids = jnp.arange(peers * depth, dtype=jnp.int32)
    match = places[None, :] == slot_ids[:, None]
    requests = jnp.sum(jnp.where(match, block_col[None, :], 0), axis=1).reshape(peers, depth)
    local_gram = jnp.dot(factor_dst.T, factor_dst, preferred_element_type=jnp.float32)
    chunk = local_gram.shape[0] // peers
    asked_row = jnp.zeros((peers, 1, width), jnp.float32).at[:, 0, :depth].set(requests.astype(jnp.float32))
    first = jnp.concatenate([local_gram.reshape(peers, chunk, width), asked_row], axis=1)
    first = lax.all_to_all(first, "dst", split_axis=0, concat_axis=0, tiled=True)
    gram_rows = jnp.sum(first[:, :chunk, :], axis=0)
    asked = first[:, chunk, :depth].astype(jnp.int32)
    spread = jnp.broadcast_to(gram_rows[None], (peers, chunk, width))
    gram_left = lax.all_to_all(spread, "dst", split_axis=0, concat_axis=0, tiled=True)
    gram_left = gram_left.reshape(peers * chunk, width)
    tiles_dst = factor_dst.reshape(factor_dst.shape[0] // edge, edge, width)
    outgoing = tiles_dst[asked.reshape(peers * depth)].reshape(peers, depth, edge, width)
    received = lax.all_to_all(outgoing, "dst", split_axis=0, concat_axis=0, tiled=True)
    received = received.reshape(peers * depth, edge, width)

    row_blocks = factor_old.shape[0] * peers // edge
    partial_sum = block_products(slab_blocks, received, places, block_row, factor_slab, row_blocks)
    partial_sum = partial_sum.reshape(row_blocks * edge, width)
    partial_sum, gram_left = lax.optimization_barrier((partial_sum, gram_left))
    summed_rows = scatter_sum(partial_sum, peers)

    gram_right = jnp.dot(factor_slab.T, factor_slab, preferred_element_type=jnp.float32)
    gram = gram_left * gram_right + RIDGE * jnp.eye(width, dtype=jnp.float32)
    inverse = ridge_inverse(gram)
    target = summed_rows + RIDGE * factor_old
    return jnp.dot(target, inverse, precision=lax.Precision.HIGHEST)


def solution(mesh):
    placed = (
        P(("src", "dst"), None, None),
        P(("src", "dst"), None),
        P(("src", "dst")),
        P(("src", "dst")),
        P("dst", None),
        P(),
        P(("src", "dst"), None),
    )
    return jax.shard_map(
        shards, mesh=mesh, in_specs=placed, out_specs=P(("src", "dst"), None), check_vma=False
    )
```

```python
import functools

import jax
import jax.numpy as jnp
from jax import lax
from jax.experimental import pallas as pl
from jax.experimental.pallas import tpu as pltpu
from jax.sharding import PartitionSpec as P

RIDGE = 0.1


def mttkrp_kernel(rows_ref, places_ref, x_ref, left_ref, slab_ref, out_ref, kr_ref):
    step = pl.program_id(0)

    @pl.when(step == 0)
    def _():
        out_ref[...] = jnp.zeros_like(out_ref)

    left = left_ref[0]
    slab = slab_ref[...]
    edge = left.shape[0]
    bins = slab.shape[0]
    for b in range(edge):
        kr_ref[pl.ds(b * bins, bins), :] = (left[b : b + 1, :] * slab).astype(kr_ref.dtype)
    prod = jnp.dot(x_ref[0], kr_ref[...], preferred_element_type=jnp.float32)
    row = rows_ref[step]
    out_ref[row] = out_ref[row] + prod


def block_products(slab_blocks, received, places, block_row, factor_slab, row_blocks, depth):
    count, edge, depth_k = slab_blocks.shape
    width = received.shape[2]
    grid_spec = pltpu.PrefetchScalarGridSpec(
        num_scalar_prefetch=2,
        grid=(count,),
        in_specs=[
            pl.BlockSpec((1, edge, depth_k), lambda i, rows, pl_: (i, 0, 0)),
            pl.BlockSpec((1, edge, width), lambda i, rows, pl_: (pl_[i] // depth, pl_[i] % depth, 0)),
            pl.BlockSpec(factor_slab.shape, lambda i, rows, pl_: (0, 0)),
        ],
        out_specs=pl.BlockSpec((row_blocks, edge, width), lambda i, rows, pl_: (0, 0, 0)),
        scratch_shapes=[pltpu.VMEM((depth_k, width), jnp.bfloat16)],
    )
    flops = 2 * count * edge * depth_k * width
    return pl.pallas_call(
        mttkrp_kernel,
        grid_spec=grid_spec,
        out_shape=jax.ShapeDtypeStruct((row_blocks, edge, width), jnp.float32),
        compiler_params=pltpu.CompilerParams(
            dimension_semantics=("arbitrary",), vmem_limit_bytes=48 * 1024 * 1024
        ),
        cost_estimate=pl.CostEstimate(
            flops=flops,
            bytes_accessed=slab_blocks.size * 2 + count * edge * width * 2 + row_blocks * edge * width * 4,
            transcendentals=0,
        ),
    )(block_row, places, slab_blocks, received, factor_slab)


def scatter_sum(rows, peers):
    pieces = rows.reshape(peers, rows.shape[0] // peers, rows.shape[1])
    arrived = lax.all_to_all(pieces, "dst", split_axis=0, concat_axis=0, tiled=True)
    return jnp.sum(arrived, axis=0)


def split_bf16(values):
    high = lax.reduce_precision(values, exponent_bits=8, mantissa_bits=7)
    rest = values - high
    middle = lax.reduce_precision(rest, exponent_bits=8, mantissa_bits=7)
    low = rest - middle
    return jnp.concatenate([high, middle, low], axis=0).astype(jnp.bfloat16)


def ridge_inverse(gram):
    eye = jnp.eye(gram.shape[0], dtype=jnp.float32)
    start = eye / jnp.max(jnp.sum(jnp.abs(gram), axis=1))

    def going(state):
        steps, _, norm = state
        return (norm >= 1e-3) & (steps < 64)

    def step(state):
        steps, inverse, _ = state
        residual = eye - jnp.dot(gram, inverse, precision=lax.Precision.HIGHEST)
        norm = jnp.max(jnp.sum(jnp.abs(residual), axis=1))
        inverse = inverse + jnp.dot(inverse, residual, precision=lax.Precision.HIGHEST)
        return steps + 1, inverse, norm

    inverse = start
    for _ in range(9):
        inverse = inverse + jnp.dot(
            inverse, eye - jnp.dot(gram, inverse, precision=lax.Precision.HIGHEST), precision=lax.Precision.HIGHEST
        )
    _, inverse, _ = lax.while_loop(going, step, (jnp.int32(0), inverse, jnp.float32(2.0)))
    return inverse


def shards(slab_blocks, owner_column, block_row, block_col, factor_dst, factor_slab, factor_old):
    peers = lax.axis_size("dst")
    count = slab_blocks.shape[0]
    edge = slab_blocks.shape[1]
    width = factor_dst.shape[1]
    depth = max(2, 4 * count // peers)
    owners = owner_column[:, 0]
    order = jnp.arange(count, dtype=jnp.int32)
    same = (owners[:, None] == owners[None, :]) & (order[None, :] < order[:, None])
    places = owners * depth + jnp.sum(same.astype(jnp.int32), axis=1)
    slot_ids = jnp.arange(peers * depth, dtype=jnp.int32)
    match = places[None, :] == slot_ids[:, None]
    requests = jnp.sum(jnp.where(match, block_col[None, :], 0), axis=1).reshape(peers, depth)
    local_gram = jnp.dot(factor_dst.T, factor_dst, preferred_element_type=jnp.float32)
    chunk = local_gram.shape[0] // peers
    asked_row = jnp.zeros((peers, 1, width), jnp.float32).at[:, 0, :depth].set(requests.astype(jnp.float32))
    first = jnp.concatenate([local_gram.reshape(peers, chunk, width), asked_row], axis=1)
    first = lax.all_to_all(first, "dst", split_axis=0, concat_axis=0, tiled=True)
    gram_rows = jnp.sum(first[:, :chunk, :], axis=0)
    asked = first[:, chunk, :depth].astype(jnp.int32)
    parts = split_bf16(gram_rows)
    spread = jnp.broadcast_to(parts[None], (peers,) + parts.shape)
    tiles_dst = factor_dst.reshape(factor_dst.shape[0] // edge, edge, width)
    outgoing = tiles_dst[asked.reshape(peers * depth)].reshape(peers, depth * edge, width)
    outgoing = jnp.concatenate([outgoing, spread], axis=1)
    arrived = lax.all_to_all(outgoing, "dst", split_axis=0, concat_axis=0, tiled=True)
    pieces = arrived[:, depth * edge :].astype(jnp.float32).reshape(peers, 3, chunk, width)
    gram_left = (pieces[:, 0] + pieces[:, 1] + pieces[:, 2]).reshape(peers * chunk, width)

    row_blocks = factor_old.shape[0] * peers // edge
    partial_sum = block_products(slab_blocks, arrived, places, block_row, factor_slab, row_blocks, depth)
    partial_sum = partial_sum.reshape(row_blocks * edge, width)
    partial_sum, gram_left = lax.optimization_barrier((partial_sum, gram_left))
    summed_rows = scatter_sum(partial_sum, peers)

    gram_right = jnp.dot(factor_slab.T, factor_slab, preferred_element_type=jnp.float32)
    gram = gram_left * gram_right + RIDGE * jnp.eye(width, dtype=jnp.float32)
    inverse = ridge_inverse(gram)
    target = summed_rows + RIDGE * factor_old
    return jnp.dot(target, inverse, precision=lax.Precision.HIGHEST)


def solution(mesh):
    placed = (
        P(("src", "dst"), None, None),
        P(("src", "dst"), None),
        P(("src", "dst")),
        P(("src", "dst")),
        P("dst", None),
        P(),
        P(("src", "dst"), None),
    )
    return jax.shard_map(
        shards, mesh=mesh, in_specs=placed, out_specs=P(("src", "dst"), None), check_vma=False
    )
```

```python
import functools

import jax
import jax.numpy as jnp
from jax import lax
from jax.experimental import pallas as pl
from jax.experimental.pallas import tpu as pltpu
from jax.sharding import PartitionSpec as P

RIDGE = 0.1


def mttkrp_kernel(rows_ref, places_ref, x_ref, left_a_ref, left_b_ref, slab_ref, out_ref, kr_ref):
    step = pl.program_id(0)

    @pl.when(step == 0)
    def _():
        out_ref[...] = jnp.zeros_like(out_ref)

    slab = slab_ref[...]
    bins = slab.shape[0]
    for half, left_ref in enumerate((left_a_ref, left_b_ref)):
        left = left_ref[0]
        for b in range(left.shape[0]):
            kr_ref[pl.ds(b * bins, bins), :] = (left[b : b + 1, :] * slab).astype(kr_ref.dtype)
        prod = jnp.dot(x_ref[half], kr_ref[...], preferred_element_type=jnp.float32)
        row = rows_ref[2 * step + half]
        out_ref[row] = out_ref[row] + prod


def block_products(slab_blocks, received, places, block_row, factor_slab, row_blocks):
    count, edge, depth_k = slab_blocks.shape
    width = received.shape[2]
    grid_spec = pltpu.PrefetchScalarGridSpec(
        num_scalar_prefetch=2,
        grid=(count // 2,),
        in_specs=[
            pl.BlockSpec((2, edge, depth_k), lambda i, rows, pl_: (i, 0, 0)),
            pl.BlockSpec((1, received.shape[1], width), lambda i, rows, pl_: (pl_[2 * i], 0, 0)),
            pl.BlockSpec((1, received.shape[1], width), lambda i, rows, pl_: (pl_[2 * i + 1], 0, 0)),
            pl.BlockSpec(factor_slab.shape, lambda i, rows, pl_: (0, 0)),
        ],
        out_specs=pl.BlockSpec((row_blocks, edge, width), lambda i, rows, pl_: (0, 0, 0)),
        scratch_shapes=[pltpu.VMEM((depth_k, width), jnp.bfloat16)],
    )
    flops = 2 * count * edge * depth_k * width
    return pl.pallas_call(
        mttkrp_kernel,
        grid_spec=grid_spec,
        out_shape=jax.ShapeDtypeStruct((row_blocks, edge, width), jnp.float32),
        compiler_params=pltpu.CompilerParams(
            dimension_semantics=("arbitrary",), vmem_limit_bytes=48 * 1024 * 1024
        ),
        cost_estimate=pl.CostEstimate(
            flops=flops,
            bytes_accessed=slab_blocks.size * 2 + count * edge * width * 2 + row_blocks * edge * width * 4,
            transcendentals=0,
        ),
    )(block_row, places, slab_blocks, received, received, factor_slab)


def scatter_sum(rows, peers):
    pieces = rows.reshape(peers, rows.shape[0] // peers, rows.shape[1])
    arrived = lax.all_to_all(pieces, "dst", split_axis=0, concat_axis=0, tiled=True)
    return jnp.sum(arrived, axis=0)


def ridge_inverse(gram):
    eye = jnp.eye(gram.shape[0], dtype=jnp.float32)
    start = eye / jnp.max(jnp.sum(jnp.abs(gram), axis=1))

    def going(state):
        steps, _, norm = state
        return (norm >= 1e-3) & (steps < 64)

    def step(state):
        steps, inverse, _ = state
        residual = eye - jnp.dot(gram, inverse, precision=lax.Precision.HIGHEST)
        norm = jnp.max(jnp.sum(jnp.abs(residual), axis=1))
        inverse = inverse + jnp.dot(inverse, residual, precision=lax.Precision.HIGHEST)
        return steps + 1, inverse, norm

    inverse = start
    for _ in range(9):
        inverse = inverse + jnp.dot(
            inverse, eye - jnp.dot(gram, inverse, precision=lax.Precision.HIGHEST), precision=lax.Precision.HIGHEST
        )
    _, inverse, _ = lax.while_loop(going, step, (jnp.int32(0), inverse, jnp.float32(2.0)))
    return inverse


def shards(slab_blocks, owner_column, block_row, block_col, factor_dst, factor_slab, factor_old):
    peers = lax.axis_size("dst")
    count = slab_blocks.shape[0]
    edge = slab_blocks.shape[1]
    width = factor_dst.shape[1]
    depth = max(2, 4 * count // peers)
    owners = owner_column[:, 0]
    order = jnp.arange(count, dtype=jnp.int32)
    same = (owners[:, None] == owners[None, :]) & (order[None, :] < order[:, None])
    places = owners * depth + jnp.sum(same.astype(jnp.int32), axis=1)
    slot_ids = jnp.arange(peers * depth, dtype=jnp.int32)
    match = places[None, :] == slot_ids[:, None]
    requests = jnp.sum(jnp.where(match, block_col[None, :], 0), axis=1).reshape(peers, depth)
    local_gram = jnp.dot(factor_dst.T, factor_dst, preferred_element_type=jnp.float32)
    chunk = local_gram.shape[0] // peers
    asked_row = jnp.zeros((peers, 1, width), jnp.float32).at[:, 0, :depth].set(requests.astype(jnp.float32))
    first = jnp.concatenate([local_gram.reshape(peers, chunk, width), asked_row], axis=1)
    first = lax.all_to_all(first, "dst", split_axis=0, concat_axis=0, tiled=True)
    gram_rows = jnp.sum(first[:, :chunk, :], axis=0)
    asked = first[:, chunk, :depth].astype(jnp.int32)
    spread = jnp.broadcast_to(gram_rows[None], (peers, chunk, width))
    gram_left = lax.all_to_all(spread, "dst", split_axis=0, concat_axis=0, tiled=True)
    gram_left = gram_left.reshape(peers * chunk, width)
    tiles_dst = factor_dst.reshape(factor_dst.shape[0] // edge, edge, width)
    outgoing = tiles_dst[asked.reshape(peers * depth)].reshape(peers, depth, edge, width)
    received = lax.all_to_all(outgoing, "dst", split_axis=0, concat_axis=0, tiled=True)
    received = received.reshape(peers * depth, edge, width)

    row_blocks = factor_old.shape[0] * peers // edge
    partial_sum = block_products(slab_blocks, received, places, block_row, factor_slab, row_blocks)
    partial_sum = partial_sum.reshape(row_blocks * edge, width)
    partial_sum, gram_left = lax.optimization_barrier((partial_sum, gram_left))
    summed_rows = scatter_sum(partial_sum, peers)

    gram_right = jnp.dot(factor_slab.T, factor_slab, preferred_element_type=jnp.float32)
    gram = gram_left * gram_right + RIDGE * jnp.eye(width, dtype=jnp.float32)
    inverse = ridge_inverse(gram)
    target = summed_rows + RIDGE * factor_old
    return jnp.dot(target, inverse, precision=lax.Precision.HIGHEST)


def solution(mesh):
    placed = (
        P(("src", "dst"), None, None),
        P(("src", "dst"), None),
        P(("src", "dst")),
        P(("src", "dst")),
        P("dst", None),
        P(),
        P(("src", "dst"), None),
    )
    return jax.shard_map(
        shards, mesh=mesh, in_specs=placed, out_specs=P(("src", "dst"), None), check_vma=False
    )
```

```python
import functools

import jax
import jax.numpy as jnp
from jax import lax
from jax.experimental import pallas as pl
from jax.experimental.pallas import tpu as pltpu
from jax.sharding import PartitionSpec as P

RIDGE = 0.1


GROUP = 4


def mttkrp_kernel(rows_ref, places_ref, x_ref, *refs):
    left_refs, (slab_ref, out_ref, kr_ref) = refs[:GROUP], refs[GROUP:]
    step = pl.program_id(0)

    @pl.when(step == 0)
    def _():
        out_ref[...] = jnp.zeros_like(out_ref)

    slab = slab_ref[...]
    bins = slab.shape[0]
    for part, left_ref in enumerate(left_refs):
        left = left_ref[0]
        for b in range(left.shape[0]):
            kr_ref[pl.ds(b * bins, bins), :] = (left[b : b + 1, :] * slab).astype(kr_ref.dtype)
        prod = jnp.dot(x_ref[part], kr_ref[...], preferred_element_type=jnp.float32)
        row = rows_ref[GROUP * step + part]
        out_ref[row] = out_ref[row] + prod


def left_spec(shape, part):
    return pl.BlockSpec(shape, lambda i, rows, pl_: (pl_[GROUP * i + part], 0, 0))


def block_products(slab_blocks, received, places, block_row, factor_slab, row_blocks):
    count, edge, depth_k = slab_blocks.shape
    width = received.shape[2]
    grid_spec = pltpu.PrefetchScalarGridSpec(
        num_scalar_prefetch=2,
        grid=(count // GROUP,),
        in_specs=[pl.BlockSpec((GROUP, edge, depth_k), lambda i, rows, pl_: (i, 0, 0))]
        + [left_spec((1, received.shape[1], width), part) for part in range(GROUP)]
        + [pl.BlockSpec(factor_slab.shape, lambda i, rows, pl_: (0, 0))],
        out_specs=pl.BlockSpec((row_blocks, edge, width), lambda i, rows, pl_: (0, 0, 0)),
        scratch_shapes=[pltpu.VMEM((depth_k, width), jnp.bfloat16)],
    )
    flops = 2 * count * edge * depth_k * width
    return pl.pallas_call(
        mttkrp_kernel,
        grid_spec=grid_spec,
        out_shape=jax.ShapeDtypeStruct((row_blocks, edge, width), jnp.float32),
        compiler_params=pltpu.CompilerParams(
            dimension_semantics=("arbitrary",), vmem_limit_bytes=48 * 1024 * 1024
        ),
        cost_estimate=pl.CostEstimate(
            flops=flops,
            bytes_accessed=slab_blocks.size * 2 + count * edge * width * 2 + row_blocks * edge * width * 4,
            transcendentals=0,
        ),
    )(block_row, places, slab_blocks, *([received] * GROUP), factor_slab)


def scatter_sum(rows, peers):
    pieces = rows.reshape(peers, rows.shape[0] // peers, rows.shape[1])
    arrived = lax.all_to_all(pieces, "dst", split_axis=0, concat_axis=0, tiled=True)
    return jnp.sum(arrived, axis=0)


def ridge_inverse(gram):
    eye = jnp.eye(gram.shape[0], dtype=jnp.float32)
    start = eye / jnp.max(jnp.sum(jnp.abs(gram), axis=1))

    def going(state):
        steps, _, norm = state
        return (norm >= 1e-3) & (steps < 64)

    def step(state):
        steps, inverse, _ = state
        residual = eye - jnp.dot(gram, inverse, precision=lax.Precision.HIGHEST)
        norm = jnp.max(jnp.sum(jnp.abs(residual), axis=1))
        inverse = inverse + jnp.dot(inverse, residual, precision=lax.Precision.HIGHEST)
        return steps + 1, inverse, norm

    inverse = start
    for _ in range(9):
        inverse = inverse + jnp.dot(
            inverse, eye - jnp.dot(gram, inverse, precision=lax.Precision.HIGHEST), precision=lax.Precision.HIGHEST
        )
    _, inverse, _ = lax.while_loop(going, step, (jnp.int32(0), inverse, jnp.float32(2.0)))
    return inverse


def shards(slab_blocks, owner_column, block_row, block_col, factor_dst, factor_slab, factor_old):
    peers = lax.axis_size("dst")
    count = slab_blocks.shape[0]
    edge = slab_blocks.shape[1]
    width = factor_dst.shape[1]
    depth = max(2, 4 * count // peers)
    owners = owner_column[:, 0]
    order = jnp.arange(count, dtype=jnp.int32)
    same = (owners[:, None] == owners[None, :]) & (order[None, :] < order[:, None])
    places = owners * depth + jnp.sum(same.astype(jnp.int32), axis=1)
    slot_ids = jnp.arange(peers * depth, dtype=jnp.int32)
    match = places[None, :] == slot_ids[:, None]
    requests = jnp.sum(jnp.where(match, block_col[None, :], 0), axis=1).reshape(peers, depth)
    local_gram = jnp.dot(factor_dst.T, factor_dst, preferred_element_type=jnp.float32)
    chunk = local_gram.shape[0] // peers
    asked_row = jnp.zeros((peers, 1, width), jnp.float32).at[:, 0, :depth].set(requests.astype(jnp.float32))
    first = jnp.concatenate([local_gram.reshape(peers, chunk, width), asked_row], axis=1)
    first = lax.all_to_all(first, "dst", split_axis=0, concat_axis=0, tiled=True)
    gram_rows = jnp.sum(first[:, :chunk, :], axis=0)
    asked = first[:, chunk, :depth].astype(jnp.int32)
    spread = jnp.broadcast_to(gram_rows[None], (peers, chunk, width))
    gram_left = lax.all_to_all(spread, "dst", split_axis=0, concat_axis=0, tiled=True)
    gram_left = gram_left.reshape(peers * chunk, width)
    tiles_dst = factor_dst.reshape(factor_dst.shape[0] // edge, edge, width)
    outgoing = tiles_dst[asked.reshape(peers * depth)].reshape(peers, depth, edge, width)
    received = lax.all_to_all(outgoing, "dst", split_axis=0, concat_axis=0, tiled=True)
    received = received.reshape(peers * depth, edge, width)

    row_blocks = factor_old.shape[0] * peers // edge
    partial_sum = block_products(slab_blocks, received, places, block_row, factor_slab, row_blocks)
    partial_sum = partial_sum.reshape(row_blocks * edge, width)
    partial_sum, gram_left = lax.optimization_barrier((partial_sum, gram_left))
    summed_rows = scatter_sum(partial_sum, peers)

    gram_right = jnp.dot(factor_slab.T, factor_slab, preferred_element_type=jnp.float32)
    gram = gram_left * gram_right + RIDGE * jnp.eye(width, dtype=jnp.float32)
    inverse = ridge_inverse(gram)
    target = summed_rows + RIDGE * factor_old
    return jnp.dot(target, inverse, precision=lax.Precision.HIGHEST)


def solution(mesh):
    placed = (
        P(("src", "dst"), None, None),
        P(("src", "dst"), None),
        P(("src", "dst")),
        P(("src", "dst")),
        P("dst", None),
        P(),
        P(("src", "dst"), None),
    )
    return jax.shard_map(
        shards, mesh=mesh, in_specs=placed, out_specs=P(("src", "dst"), None), check_vma=False
    )
```

```python
import functools

import jax
import jax.numpy as jnp
from jax import lax
from jax.experimental import pallas as pl
from jax.experimental.pallas import tpu as pltpu
from jax.sharding import PartitionSpec as P

RIDGE = 0.1


GROUP = 4


def mttkrp_kernel(rows_ref, places_ref, x_ref, *refs):
    left_refs, (slab_ref, out_ref, kr_ref) = refs[:GROUP], refs[GROUP:]
    step = pl.program_id(0)

    @pl.when(step == 0)
    def _():
        out_ref[...] = jnp.zeros_like(out_ref)

    slab = slab_ref[...]
    bins = slab.shape[0]
    for part, left_ref in enumerate(left_refs):
        left = left_ref[0]
        for b in range(left.shape[0]):
            kr_ref[pl.ds(b * bins, bins), :] = (left[b : b + 1, :] * slab).astype(kr_ref.dtype)
        prod = jnp.dot(x_ref[part], kr_ref[...], preferred_element_type=jnp.float32)
        row = rows_ref[GROUP * step + part]
        out_ref[row] = out_ref[row] + prod


def left_spec(shape, part):
    return pl.BlockSpec(shape, lambda i, rows, pl_: (pl_[GROUP * i + part], 0, 0))


def block_products(slab_blocks, received, places, block_row, factor_slab, row_blocks):
    count, edge, depth_k = slab_blocks.shape
    width = received.shape[2]
    grid_spec = pltpu.PrefetchScalarGridSpec(
        num_scalar_prefetch=2,
        grid=(count // GROUP,),
        in_specs=[pl.BlockSpec((GROUP, edge, depth_k), lambda i, rows, pl_: (i, 0, 0))]
        + [left_spec((1, received.shape[1], width), part) for part in range(GROUP)]
        + [pl.BlockSpec(factor_slab.shape, lambda i, rows, pl_: (0, 0))],
        out_specs=pl.BlockSpec((row_blocks, edge, width), lambda i, rows, pl_: (0, 0, 0)),
        scratch_shapes=[pltpu.VMEM((depth_k, width), jnp.bfloat16)],
    )
    flops = 2 * count * edge * depth_k * width
    return pl.pallas_call(
        mttkrp_kernel,
        grid_spec=grid_spec,
        out_shape=jax.ShapeDtypeStruct((row_blocks, edge, width), jnp.float32),
        compiler_params=pltpu.CompilerParams(
            dimension_semantics=("arbitrary",), vmem_limit_bytes=48 * 1024 * 1024
        ),
        cost_estimate=pl.CostEstimate(
            flops=flops,
            bytes_accessed=slab_blocks.size * 2 + count * edge * width * 2 + row_blocks * edge * width * 4,
            transcendentals=0,
        ),
    )(block_row, places, slab_blocks, *([received] * GROUP), factor_slab)


def scatter_sum(rows, peers):
    pieces = rows.reshape(peers, rows.shape[0] // peers, rows.shape[1])
    arrived = lax.all_to_all(pieces, "dst", split_axis=0, concat_axis=0, tiled=True)
    return jnp.sum(arrived, axis=0)


def gather_rows(rows, peers):
    me = lax.axis_index("dst")
    held = rows
    distance = 1
    while distance < peers:
        pairs = [(i, i ^ distance) for i in range(peers)]
        other = lax.ppermute(held, "dst", perm=pairs)
        low = (me & distance) == 0
        held = jnp.where(low, jnp.concatenate([held, other]), jnp.concatenate([other, held]))
        distance *= 2
    return held


def ridge_inverse(gram):
    eye = jnp.eye(gram.shape[0], dtype=jnp.float32)
    start = eye / jnp.max(jnp.sum(jnp.abs(gram), axis=1))

    def going(state):
        steps, _, norm = state
        return (norm >= 1e-3) & (steps < 64)

    def step(state):
        steps, inverse, _ = state
        residual = eye - jnp.dot(gram, inverse, precision=lax.Precision.HIGHEST)
        norm = jnp.max(jnp.sum(jnp.abs(residual), axis=1))
        inverse = inverse + jnp.dot(inverse, residual, precision=lax.Precision.HIGHEST)
        return steps + 1, inverse, norm

    inverse = start
    for _ in range(9):
        inverse = inverse + jnp.dot(
            inverse, eye - jnp.dot(gram, inverse, precision=lax.Precision.HIGHEST), precision=lax.Precision.HIGHEST
        )
    _, inverse, _ = lax.while_loop(going, step, (jnp.int32(0), inverse, jnp.float32(2.0)))
    return inverse


def shards(slab_blocks, owner_column, block_row, block_col, factor_dst, factor_slab, factor_old):
    peers = lax.axis_size("dst")
    count = slab_blocks.shape[0]
    edge = slab_blocks.shape[1]
    width = factor_dst.shape[1]
    depth = max(2, 4 * count // peers)
    owners = owner_column[:, 0]
    order = jnp.arange(count, dtype=jnp.int32)
    same = (owners[:, None] == owners[None, :]) & (order[None, :] < order[:, None])
    places = owners * depth + jnp.sum(same.astype(jnp.int32), axis=1)
    slot_ids = jnp.arange(peers * depth, dtype=jnp.int32)
    match = places[None, :] == slot_ids[:, None]
    requests = jnp.sum(jnp.where(match, block_col[None, :], 0), axis=1).reshape(peers, depth)
    local_gram = jnp.dot(factor_dst.T, factor_dst, preferred_element_type=jnp.float32)
    chunk = local_gram.shape[0] // peers
    asked_row = jnp.zeros((peers, 1, width), jnp.float32).at[:, 0, :depth].set(requests.astype(jnp.float32))
    first = jnp.concatenate([local_gram.reshape(peers, chunk, width), asked_row], axis=1)
    first = lax.all_to_all(first, "dst", split_axis=0, concat_axis=0, tiled=True)
    gram_rows = jnp.sum(first[:, :chunk, :], axis=0)
    asked = first[:, chunk, :depth].astype(jnp.int32)
    tiles_dst = factor_dst.reshape(factor_dst.shape[0] // edge, edge, width)
    outgoing = tiles_dst[asked.reshape(peers * depth)].reshape(peers, depth, edge, width)
    received = lax.all_to_all(outgoing, "dst", split_axis=0, concat_axis=0, tiled=True)
    gram_rows, outgoing = lax.optimization_barrier((gram_rows, outgoing))
    gram_left = gather_rows(gram_rows, peers)
    received = received.reshape(peers * depth, edge, width)

    row_blocks = factor_old.shape[0] * peers // edge
    partial_sum = block_products(slab_blocks, received, places, block_row, factor_slab, row_blocks)
    partial_sum = partial_sum.reshape(row_blocks * edge, width)
    summed_rows = scatter_sum(partial_sum, peers)

    gram_right = jnp.dot(factor_slab.T, factor_slab, preferred_element_type=jnp.float32)
    gram = gram_left * gram_right + RIDGE * jnp.eye(width, dtype=jnp.float32)
    inverse = ridge_inverse(gram)
    target = summed_rows + RIDGE * factor_old
    return jnp.dot(target, inverse, precision=lax.Precision.HIGHEST)


def solution(mesh):
    placed = (
        P(("src", "dst"), None, None),
        P(("src", "dst"), None),
        P(("src", "dst")),
        P(("src", "dst")),
        P("dst", None),
        P(),
        P(("src", "dst"), None),
    )
    return jax.shard_map(
        shards, mesh=mesh, in_specs=placed, out_specs=P(("src", "dst"), None), check_vma=False
    )
```

```python
import functools

import jax
import jax.numpy as jnp
from jax import lax
from jax.experimental import pallas as pl
from jax.experimental.pallas import tpu as pltpu
from jax.sharding import PartitionSpec as P

RIDGE = 0.1


GROUP = 4


def mttkrp_kernel(rows_ref, places_ref, x_ref, *refs):
    left_refs, (slab_ref, out_ref, kr_ref) = refs[:GROUP], refs[GROUP:]
    step = pl.program_id(0)

    @pl.when(step == 0)
    def _():
        out_ref[...] = jnp.zeros_like(out_ref)

    slab = slab_ref[...]
    bins = slab.shape[0]
    for part, left_ref in enumerate(left_refs):
        left = left_ref[0]
        for b in range(left.shape[0]):
            kr_ref[pl.ds(b * bins, bins), :] = (left[b : b + 1, :] * slab).astype(kr_ref.dtype)
        prod = jnp.dot(x_ref[part], kr_ref[...], preferred_element_type=jnp.float32)
        row = rows_ref[GROUP * step + part]
        out_ref[row] = out_ref[row] + prod


def left_spec(shape, part):
    return pl.BlockSpec(shape, lambda i, rows, pl_: (pl_[GROUP * i + part], 0, 0))


def block_products(slab_blocks, received, places, block_row, factor_slab, row_blocks):
    count, edge, depth_k = slab_blocks.shape
    width = received.shape[2]
    grid_spec = pltpu.PrefetchScalarGridSpec(
        num_scalar_prefetch=2,
        grid=(count // GROUP,),
        in_specs=[pl.BlockSpec((GROUP, edge, depth_k), lambda i, rows, pl_: (i, 0, 0))]
        + [left_spec((1, received.shape[1], width), part) for part in range(GROUP)]
        + [pl.BlockSpec(factor_slab.shape, lambda i, rows, pl_: (0, 0))],
        out_specs=pl.BlockSpec((row_blocks, edge, width), lambda i, rows, pl_: (0, 0, 0)),
        scratch_shapes=[pltpu.VMEM((depth_k, width), jnp.bfloat16)],
    )
    flops = 2 * count * edge * depth_k * width
    return pl.pallas_call(
        mttkrp_kernel,
        grid_spec=grid_spec,
        out_shape=jax.ShapeDtypeStruct((row_blocks, edge, width), jnp.float32),
        compiler_params=pltpu.CompilerParams(
            dimension_semantics=("arbitrary",), vmem_limit_bytes=48 * 1024 * 1024
        ),
        cost_estimate=pl.CostEstimate(
            flops=flops,
            bytes_accessed=slab_blocks.size * 2 + count * edge * width * 2 + row_blocks * edge * width * 4,
            transcendentals=0,
        ),
    )(block_row, places, slab_blocks, *([received] * GROUP), factor_slab)


def scatter_sum(rows, peers):
    pieces = rows.reshape(peers, rows.shape[0] // peers, rows.shape[1])
    arrived = lax.all_to_all(pieces, "dst", split_axis=0, concat_axis=0, tiled=True)
    return jnp.sum(arrived, axis=0)


def ridge_inverse(gram):
    eye = jnp.eye(gram.shape[0], dtype=jnp.float32)
    start = eye / jnp.max(jnp.sum(jnp.abs(gram), axis=1))

    def going(state):
        steps, _, norm = state
        return (norm >= 1e-3) & (steps < 64)

    def step(state):
        steps, inverse, _ = state
        residual = eye - jnp.dot(gram, inverse, precision=lax.Precision.HIGHEST)
        norm = jnp.max(jnp.sum(jnp.abs(residual), axis=1))
        inverse = inverse + jnp.dot(inverse, residual, precision=lax.Precision.HIGHEST)
        return steps + 1, inverse, norm

    inverse = start
    for count in range(9):
        level = lax.Precision.HIGH if count < 6 else lax.Precision.HIGHEST
        inverse = inverse + jnp.dot(inverse, eye - jnp.dot(gram, inverse, precision=level), precision=level)
    _, inverse, _ = lax.while_loop(going, step, (jnp.int32(0), inverse, jnp.float32(2.0)))
    return inverse


def shards(slab_blocks, owner_column, block_row, block_col, factor_dst, factor_slab, factor_old):
    peers = lax.axis_size("dst")
    count = slab_blocks.shape[0]
    edge = slab_blocks.shape[1]
    width = factor_dst.shape[1]
    depth = max(2, 4 * count // peers)
    owners = owner_column[:, 0]
    order = jnp.arange(count, dtype=jnp.int32)
    same = (owners[:, None] == owners[None, :]) & (order[None, :] < order[:, None])
    places = owners * depth + jnp.sum(same.astype(jnp.int32), axis=1)
    slot_ids = jnp.arange(peers * depth, dtype=jnp.int32)
    match = places[None, :] == slot_ids[:, None]
    requests = jnp.sum(jnp.where(match, block_col[None, :], 0), axis=1).reshape(peers, depth)
    local_gram = jnp.dot(factor_dst.T, factor_dst, preferred_element_type=jnp.float32)
    chunk = local_gram.shape[0] // peers
    asked_row = jnp.zeros((peers, 1, width), jnp.float32).at[:, 0, :depth].set(requests.astype(jnp.float32))
    first = jnp.concatenate([local_gram.reshape(peers, chunk, width), asked_row], axis=1)
    first = lax.all_to_all(first, "dst", split_axis=0, concat_axis=0, tiled=True)
    gram_rows = jnp.sum(first[:, :chunk, :], axis=0)
    asked = first[:, chunk, :depth].astype(jnp.int32)
    spread = jnp.broadcast_to(gram_rows[None], (peers, chunk, width))
    gram_left = lax.all_to_all(spread, "dst", split_axis=0, concat_axis=0, tiled=True)
    gram_left = gram_left.reshape(peers * chunk, width)
    tiles_dst = factor_dst.reshape(factor_dst.shape[0] // edge, edge, width)
    outgoing = tiles_dst[asked.reshape(peers * depth)].reshape(peers, depth, edge, width)
    received = lax.all_to_all(outgoing, "dst", split_axis=0, concat_axis=0, tiled=True)
    received = received.reshape(peers * depth, edge, width)

    row_blocks = factor_old.shape[0] * peers // edge
    partial_sum = block_products(slab_blocks, received, places, block_row, factor_slab, row_blocks)
    partial_sum = partial_sum.reshape(row_blocks * edge, width)
    partial_sum, gram_left = lax.optimization_barrier((partial_sum, gram_left))
    summed_rows = scatter_sum(partial_sum, peers)

    gram_right = jnp.dot(factor_slab.T, factor_slab, preferred_element_type=jnp.float32)
    gram = gram_left * gram_right + RIDGE * jnp.eye(width, dtype=jnp.float32)
    inverse = ridge_inverse(gram)
    target = summed_rows + RIDGE * factor_old
    return jnp.dot(target, inverse, precision=lax.Precision.HIGHEST)


def solution(mesh):
    placed = (
        P(("src", "dst"), None, None),
        P(("src", "dst"), None),
        P(("src", "dst")),
        P(("src", "dst")),
        P("dst", None),
        P(),
        P(("src", "dst"), None),
    )
    return jax.shard_map(
        shards, mesh=mesh, in_specs=placed, out_specs=P(("src", "dst"), None), check_vma=False
    )
```

```python
import functools

import jax
import jax.numpy as jnp
from jax import lax
from jax.experimental import pallas as pl
from jax.experimental.pallas import tpu as pltpu
from jax.sharding import PartitionSpec as P

RIDGE = 0.1


GROUP = 4


def mttkrp_kernel(rows_ref, places_ref, x_ref, *refs):
    left_refs, (slab_ref, out_ref, kr_ref) = refs[:GROUP], refs[GROUP:]
    step = pl.program_id(0)

    @pl.when(step == 0)
    def _():
        out_ref[...] = jnp.zeros_like(out_ref)

    slab = slab_ref[...]
    bins = slab.shape[0]
    for part, left_ref in enumerate(left_refs):
        left = left_ref[0]
        for b in range(left.shape[0]):
            kr_ref[pl.ds(b * bins, bins), :] = (left[b : b + 1, :] * slab).astype(kr_ref.dtype)
        prod = jnp.dot(x_ref[part], kr_ref[...], preferred_element_type=jnp.float32)
        row = rows_ref[GROUP * step + part]
        out_ref[row] = out_ref[row] + prod


def left_spec(shape, part):
    return pl.BlockSpec(shape, lambda i, rows, pl_: (pl_[GROUP * i + part], 0, 0))


def block_products(slab_blocks, received, places, block_row, factor_slab, row_blocks):
    count, edge, depth_k = slab_blocks.shape
    width = received.shape[2]
    grid_spec = pltpu.PrefetchScalarGridSpec(
        num_scalar_prefetch=2,
        grid=(count // GROUP,),
        in_specs=[pl.BlockSpec((GROUP, edge, depth_k), lambda i, rows, pl_: (i, 0, 0))]
        + [left_spec((1, received.shape[1], width), part) for part in range(GROUP)]
        + [pl.BlockSpec(factor_slab.shape, lambda i, rows, pl_: (0, 0))],
        out_specs=pl.BlockSpec((row_blocks, edge, width), lambda i, rows, pl_: (0, 0, 0)),
        scratch_shapes=[pltpu.VMEM((depth_k, width), jnp.bfloat16)],
    )
    flops = 2 * count * edge * depth_k * width
    return pl.pallas_call(
        mttkrp_kernel,
        grid_spec=grid_spec,
        out_shape=jax.ShapeDtypeStruct((row_blocks, edge, width), jnp.float32),
        compiler_params=pltpu.CompilerParams(
            dimension_semantics=("arbitrary",), vmem_limit_bytes=48 * 1024 * 1024
        ),
        cost_estimate=pl.CostEstimate(
            flops=flops,
            bytes_accessed=slab_blocks.size * 2 + count * edge * width * 2 + row_blocks * edge * width * 4,
            transcendentals=0,
        ),
    )(block_row, places, slab_blocks, *([received] * GROUP), factor_slab)


def scatter_sum(rows, peers):
    pieces = rows.reshape(peers, rows.shape[0] // peers, rows.shape[1])
    arrived = lax.all_to_all(pieces, "dst", split_axis=0, concat_axis=0, tiled=True)
    return jnp.sum(arrived, axis=0)


def ridge_inverse(gram):
    eye = jnp.eye(gram.shape[0], dtype=jnp.float32)
    start = eye / jnp.max(jnp.sum(jnp.abs(gram), axis=1))

    def going(state):
        steps, _, norm = state
        return (norm >= 1e-3) & (steps < 64)

    def step(state):
        steps, inverse, _ = state
        residual = eye - jnp.dot(gram, inverse, precision=lax.Precision.HIGHEST)
        norm = jnp.max(jnp.sum(jnp.abs(residual), axis=1))
        inverse = inverse + jnp.dot(inverse, residual, precision=lax.Precision.HIGHEST)
        return steps + 1, inverse, norm

    inverse = start
    for count in range(9):
        level = lax.Precision.DEFAULT if count < 6 else lax.Precision.HIGHEST
        inverse = inverse + jnp.dot(inverse, eye - jnp.dot(gram, inverse, precision=level), precision=level)
    _, inverse, _ = lax.while_loop(going, step, (jnp.int32(0), inverse, jnp.float32(2.0)))
    return inverse


def shards(slab_blocks, owner_column, block_row, block_col, factor_dst, factor_slab, factor_old):
    peers = lax.axis_size("dst")
    count = slab_blocks.shape[0]
    edge = slab_blocks.shape[1]
    width = factor_dst.shape[1]
    depth = max(2, 4 * count // peers)
    owners = owner_column[:, 0]
    order = jnp.arange(count, dtype=jnp.int32)
    same = (owners[:, None] == owners[None, :]) & (order[None, :] < order[:, None])
    places = owners * depth + jnp.sum(same.astype(jnp.int32), axis=1)
    slot_ids = jnp.arange(peers * depth, dtype=jnp.int32)
    match = places[None, :] == slot_ids[:, None]
    requests = jnp.sum(jnp.where(match, block_col[None, :], 0), axis=1).reshape(peers, depth)
    local_gram = jnp.dot(factor_dst.T, factor_dst, preferred_element_type=jnp.float32)
    chunk = local_gram.shape[0] // peers
    asked_row = jnp.zeros((peers, 1, width), jnp.float32).at[:, 0, :depth].set(requests.astype(jnp.float32))
    first = jnp.concatenate([local_gram.reshape(peers, chunk, width), asked_row], axis=1)
    first = lax.all_to_all(first, "dst", split_axis=0, concat_axis=0, tiled=True)
    gram_rows = jnp.sum(first[:, :chunk, :], axis=0)
    asked = first[:, chunk, :depth].astype(jnp.int32)
    spread = jnp.broadcast_to(gram_rows[None], (peers, chunk, width))
    gram_left = lax.all_to_all(spread, "dst", split_axis=0, concat_axis=0, tiled=True)
    gram_left = gram_left.reshape(peers * chunk, width)
    tiles_dst = factor_dst.reshape(factor_dst.shape[0] // edge, edge, width)
    outgoing = tiles_dst[asked.reshape(peers * depth)].reshape(peers, depth, edge, width)
    received = lax.all_to_all(outgoing, "dst", split_axis=0, concat_axis=0, tiled=True)
    received = received.reshape(peers * depth, edge, width)

    row_blocks = factor_old.shape[0] * peers // edge
    partial_sum = block_products(slab_blocks, received, places, block_row, factor_slab, row_blocks)
    partial_sum = partial_sum.reshape(row_blocks * edge, width)
    partial_sum, gram_left = lax.optimization_barrier((partial_sum, gram_left))
    summed_rows = scatter_sum(partial_sum, peers)

    gram_right = jnp.dot(factor_slab.T, factor_slab, preferred_element_type=jnp.float32)
    gram = gram_left * gram_right + RIDGE * jnp.eye(width, dtype=jnp.float32)
    inverse = ridge_inverse(gram)
    target = summed_rows + RIDGE * factor_old
    return jnp.dot(target, inverse, precision=lax.Precision.HIGHEST)


def solution(mesh):
    placed = (
        P(("src", "dst"), None, None),
        P(("src", "dst"), None),
        P(("src", "dst")),
        P(("src", "dst")),
        P("dst", None),
        P(),
        P(("src", "dst"), None),
    )
    return jax.shard_map(
        shards, mesh=mesh, in_specs=placed, out_specs=P(("src", "dst"), None), check_vma=False
    )
```

```python
import functools

import jax
import jax.numpy as jnp
from jax import lax
from jax.experimental import pallas as pl
from jax.experimental.pallas import tpu as pltpu
from jax.sharding import PartitionSpec as P

RIDGE = 0.1


GROUP = 6


def mttkrp_kernel(rows_ref, places_ref, x_ref, *refs):
    left_refs, (slab_ref, out_ref, kr_ref) = refs[:GROUP], refs[GROUP:]
    step = pl.program_id(0)

    @pl.when(step == 0)
    def _():
        out_ref[...] = jnp.zeros_like(out_ref)

    slab = slab_ref[...]
    bins = slab.shape[0]
    for part, left_ref in enumerate(left_refs):
        left = left_ref[0]
        for b in range(left.shape[0]):
            kr_ref[pl.ds(b * bins, bins), :] = (left[b : b + 1, :] * slab).astype(kr_ref.dtype)
        prod = jnp.dot(x_ref[part], kr_ref[...], preferred_element_type=jnp.float32)
        row = rows_ref[GROUP * step + part]
        out_ref[row] = out_ref[row] + prod


def left_spec(shape, part):
    return pl.BlockSpec(shape, lambda i, rows, pl_: (pl_[GROUP * i + part], 0, 0))


def block_products(slab_blocks, received, places, block_row, factor_slab, row_blocks):
    count, edge, depth_k = slab_blocks.shape
    width = received.shape[2]
    grid_spec = pltpu.PrefetchScalarGridSpec(
        num_scalar_prefetch=2,
        grid=(count // GROUP,),
        in_specs=[pl.BlockSpec((GROUP, edge, depth_k), lambda i, rows, pl_: (i, 0, 0))]
        + [left_spec((1, received.shape[1], width), part) for part in range(GROUP)]
        + [pl.BlockSpec(factor_slab.shape, lambda i, rows, pl_: (0, 0))],
        out_specs=pl.BlockSpec((row_blocks, edge, width), lambda i, rows, pl_: (0, 0, 0)),
        scratch_shapes=[pltpu.VMEM((depth_k, width), jnp.bfloat16)],
    )
    flops = 2 * count * edge * depth_k * width
    return pl.pallas_call(
        mttkrp_kernel,
        grid_spec=grid_spec,
        out_shape=jax.ShapeDtypeStruct((row_blocks, edge, width), jnp.float32),
        compiler_params=pltpu.CompilerParams(
            dimension_semantics=("arbitrary",), vmem_limit_bytes=48 * 1024 * 1024
        ),
        cost_estimate=pl.CostEstimate(
            flops=flops,
            bytes_accessed=slab_blocks.size * 2 + count * edge * width * 2 + row_blocks * edge * width * 4,
            transcendentals=0,
        ),
    )(block_row, places, slab_blocks, *([received] * GROUP), factor_slab)


def scatter_sum(rows, peers):
    pieces = rows.reshape(peers, rows.shape[0] // peers, rows.shape[1])
    arrived = lax.all_to_all(pieces, "dst", split_axis=0, concat_axis=0, tiled=True)
    return jnp.sum(arrived, axis=0)


def ridge_inverse(gram):
    eye = jnp.eye(gram.shape[0], dtype=jnp.float32)
    start = eye / jnp.max(jnp.sum(jnp.abs(gram), axis=1))

    def going(state):
        steps, _, norm = state
        return (norm >= 1e-3) & (steps < 64)

    def step(state):
        steps, inverse, _ = state
        residual = eye - jnp.dot(gram, inverse, precision=lax.Precision.HIGHEST)
        norm = jnp.max(jnp.sum(jnp.abs(residual), axis=1))
        inverse = inverse + jnp.dot(inverse, residual, precision=lax.Precision.HIGHEST)
        return steps + 1, inverse, norm

    inverse = start
    for count in range(9):
        level = lax.Precision.DEFAULT if count < 6 else lax.Precision.HIGHEST
        inverse = inverse + jnp.dot(inverse, eye - jnp.dot(gram, inverse, precision=level), precision=level)
    _, inverse, _ = lax.while_loop(going, step, (jnp.int32(0), inverse, jnp.float32(2.0)))
    return inverse


def shards(slab_blocks, owner_column, block_row, block_col, factor_dst, factor_slab, factor_old):
    peers = lax.axis_size("dst")
    count = slab_blocks.shape[0]
    edge = slab_blocks.shape[1]
    width = factor_dst.shape[1]
    depth = max(2, 4 * count // peers)
    owners = owner_column[:, 0]
    order = jnp.arange(count, dtype=jnp.int32)
    same = (owners[:, None] == owners[None, :]) & (order[None, :] < order[:, None])
    places = owners * depth + jnp.sum(same.astype(jnp.int32), axis=1)
    slot_ids = jnp.arange(peers * depth, dtype=jnp.int32)
    match = places[None, :] == slot_ids[:, None]
    requests = jnp.sum(jnp.where(match, block_col[None, :], 0), axis=1).reshape(peers, depth)
    local_gram = jnp.dot(factor_dst.T, factor_dst, preferred_element_type=jnp.float32)
    chunk = local_gram.shape[0] // peers
    asked_row = jnp.zeros((peers, 1, width), jnp.float32).at[:, 0, :depth].set(requests.astype(jnp.float32))
    first = jnp.concatenate([local_gram.reshape(peers, chunk, width), asked_row], axis=1)
    first = lax.all_to_all(first, "dst", split_axis=0, concat_axis=0, tiled=True)
    gram_rows = jnp.sum(first[:, :chunk, :], axis=0)
    asked = first[:, chunk, :depth].astype(jnp.int32)
    spread = jnp.broadcast_to(gram_rows[None], (peers, chunk, width))
    gram_left = lax.all_to_all(spread, "dst", split_axis=0, concat_axis=0, tiled=True)
    gram_left = gram_left.reshape(peers * chunk, width)
    tiles_dst = factor_dst.reshape(factor_dst.shape[0] // edge, edge, width)
    outgoing = tiles_dst[asked.reshape(peers * depth)].reshape(peers, depth, edge, width)
    received = lax.all_to_all(outgoing, "dst", split_axis=0, concat_axis=0, tiled=True)
    received = received.reshape(peers * depth, edge, width)

    row_blocks = factor_old.shape[0] * peers // edge
    partial_sum = block_products(slab_blocks, received, places, block_row, factor_slab, row_blocks)
    partial_sum = partial_sum.reshape(row_blocks * edge, width)
    partial_sum, gram_left = lax.optimization_barrier((partial_sum, gram_left))
    summed_rows = scatter_sum(partial_sum, peers)

    gram_right = jnp.dot(factor_slab.T, factor_slab, preferred_element_type=jnp.float32)
    gram = gram_left * gram_right + RIDGE * jnp.eye(width, dtype=jnp.float32)
    inverse = ridge_inverse(gram)
    target = summed_rows + RIDGE * factor_old
    return jnp.dot(target, inverse, precision=lax.Precision.HIGHEST)


def solution(mesh):
    placed = (
        P(("src", "dst"), None, None),
        P(("src", "dst"), None),
        P(("src", "dst")),
        P(("src", "dst")),
        P("dst", None),
        P(),
        P(("src", "dst"), None),
    )
    return jax.shard_map(
        shards, mesh=mesh, in_specs=placed, out_specs=P(("src", "dst"), None), check_vma=False
    )
```

```python
import functools

import jax
import jax.numpy as jnp
from jax import lax
from jax.experimental import pallas as pl
from jax.experimental.pallas import tpu as pltpu
from jax.sharding import PartitionSpec as P

RIDGE = 0.1


GROUP = 4


def mttkrp_kernel(rows_ref, places_ref, x_ref, *refs):
    left_refs, (slab_ref, out_ref, kr_ref) = refs[:GROUP], refs[GROUP:]
    step = pl.program_id(0)

    @pl.when(step == 0)
    def _():
        out_ref[...] = jnp.zeros_like(out_ref)

    slab = slab_ref[...]
    bins = slab.shape[0]
    for part, left_ref in enumerate(left_refs):
        left = left_ref[0]
        for b in range(left.shape[0]):
            kr_ref[pl.ds(b * bins, bins), :] = (left[b : b + 1, :] * slab).astype(kr_ref.dtype)
        prod = jnp.dot(x_ref[part], kr_ref[...], preferred_element_type=jnp.float32)
        row = rows_ref[GROUP * step + part]
        out_ref[row] = out_ref[row] + prod


def left_spec(shape, part):
    return pl.BlockSpec(shape, lambda i, rows, pl_: (pl_[GROUP * i + part], 0, 0))


def block_products(slab_blocks, received, places, block_row, factor_slab, row_blocks):
    count, edge, depth_k = slab_blocks.shape
    width = received.shape[2]
    grid_spec = pltpu.PrefetchScalarGridSpec(
        num_scalar_prefetch=2,
        grid=(count // GROUP,),
        in_specs=[pl.BlockSpec((GROUP, edge, depth_k), lambda i, rows, pl_: (i, 0, 0))]
        + [left_spec((1, received.shape[1], width), part) for part in range(GROUP)]
        + [pl.BlockSpec(factor_slab.shape, lambda i, rows, pl_: (0, 0))],
        out_specs=pl.BlockSpec((row_blocks, edge, width), lambda i, rows, pl_: (0, 0, 0)),
        scratch_shapes=[pltpu.VMEM((depth_k, width), jnp.bfloat16)],
    )
    flops = 2 * count * edge * depth_k * width
    return pl.pallas_call(
        mttkrp_kernel,
        grid_spec=grid_spec,
        out_shape=jax.ShapeDtypeStruct((row_blocks, edge, width), jnp.float32),
        compiler_params=pltpu.CompilerParams(
            dimension_semantics=("arbitrary",), vmem_limit_bytes=48 * 1024 * 1024
        ),
        cost_estimate=pl.CostEstimate(
            flops=flops,
            bytes_accessed=slab_blocks.size * 2 + count * edge * width * 2 + row_blocks * edge * width * 4,
            transcendentals=0,
        ),
    )(block_row, places, slab_blocks, *([received] * GROUP), factor_slab)


def scatter_sum(rows, peers):
    pieces = rows.reshape(peers, rows.shape[0] // peers, rows.shape[1])
    arrived = lax.all_to_all(pieces, "dst", split_axis=0, concat_axis=0, tiled=True)
    return jnp.sum(arrived, axis=0)


def ridge_inverse(gram):
    eye = jnp.eye(gram.shape[0], dtype=jnp.float32)
    start = eye / jnp.max(jnp.sum(jnp.abs(gram), axis=1))

    def going(state):
        steps, _, norm = state
        return (norm >= 1e-3) & (steps < 64)

    def step(state):
        steps, inverse, _ = state
        residual = eye - jnp.dot(gram, inverse, precision=lax.Precision.HIGHEST)
        norm = jnp.max(jnp.sum(jnp.abs(residual), axis=1))
        inverse = inverse + jnp.dot(inverse, residual, precision=lax.Precision.HIGHEST)
        return steps + 1, inverse, norm

    inverse = start
    for _ in range(9):
        level = lax.Precision.HIGH
        inverse = inverse + jnp.dot(inverse, eye - jnp.dot(gram, inverse, precision=level), precision=level)
    _, inverse, _ = lax.while_loop(going, step, (jnp.int32(0), inverse, jnp.float32(2.0)))
    return inverse


def shards(slab_blocks, owner_column, block_row, block_col, factor_dst, factor_slab, factor_old):
    peers = lax.axis_size("dst")
    count = slab_blocks.shape[0]
    edge = slab_blocks.shape[1]
    width = factor_dst.shape[1]
    depth = max(2, 4 * count // peers)
    owners = owner_column[:, 0]
    order = jnp.arange(count, dtype=jnp.int32)
    same = (owners[:, None] == owners[None, :]) & (order[None, :] < order[:, None])
    places = owners * depth + jnp.sum(same.astype(jnp.int32), axis=1)
    slot_ids = jnp.arange(peers * depth, dtype=jnp.int32)
    match = places[None, :] == slot_ids[:, None]
    requests = jnp.sum(jnp.where(match, block_col[None, :], 0), axis=1).reshape(peers, depth)
    local_gram = jnp.dot(factor_dst.T, factor_dst, preferred_element_type=jnp.float32)
    chunk = local_gram.shape[0] // peers
    asked_row = jnp.zeros((peers, 1, width), jnp.float32).at[:, 0, :depth].set(requests.astype(jnp.float32))
    first = jnp.concatenate([local_gram.reshape(peers, chunk, width), asked_row], axis=1)
    first = lax.all_to_all(first, "dst", split_axis=0, concat_axis=0, tiled=True)
    gram_rows = jnp.sum(first[:, :chunk, :], axis=0)
    asked = first[:, chunk, :depth].astype(jnp.int32)
    spread = jnp.broadcast_to(gram_rows[None], (peers, chunk, width))
    gram_left = lax.all_to_all(spread, "dst", split_axis=0, concat_axis=0, tiled=True)
    gram_left = gram_left.reshape(peers * chunk, width)
    tiles_dst = factor_dst.reshape(factor_dst.shape[0] // edge, edge, width)
    outgoing = tiles_dst[asked.reshape(peers * depth)].reshape(peers, depth, edge, width)
    received = lax.all_to_all(outgoing, "dst", split_axis=0, concat_axis=0, tiled=True)
    received = received.reshape(peers * depth, edge, width)

    row_blocks = factor_old.shape[0] * peers // edge
    partial_sum = block_products(slab_blocks, received, places, block_row, factor_slab, row_blocks)
    partial_sum = partial_sum.reshape(row_blocks * edge, width)
    partial_sum, gram_left = lax.optimization_barrier((partial_sum, gram_left))
    summed_rows = scatter_sum(partial_sum, peers)

    gram_right = jnp.dot(factor_slab.T, factor_slab, preferred_element_type=jnp.float32)
    gram = gram_left * gram_right + RIDGE * jnp.eye(width, dtype=jnp.float32)
    inverse = ridge_inverse(gram)
    target = summed_rows + RIDGE * factor_old
    return jnp.dot(target, inverse, precision=lax.Precision.HIGHEST)


def solution(mesh):
    placed = (
        P(("src", "dst"), None, None),
        P(("src", "dst"), None),
        P(("src", "dst")),
        P(("src", "dst")),
        P("dst", None),
        P(),
        P(("src", "dst"), None),
    )
    return jax.shard_map(
        shards, mesh=mesh, in_specs=placed, out_specs=P(("src", "dst"), None), check_vma=False
    )
```

```python
import functools

import jax
import jax.numpy as jnp
from jax import lax
from jax.experimental import pallas as pl
from jax.experimental.pallas import tpu as pltpu
from jax.sharding import PartitionSpec as P

RIDGE = 0.1


GROUP = 4


def mttkrp_kernel(rows_ref, places_ref, x_ref, *refs):
    left_refs, (slab_ref, out_ref, kr_ref) = refs[:GROUP], refs[GROUP:]
    step = pl.program_id(0)

    @pl.when(step == 0)
    def _():
        out_ref[...] = jnp.zeros_like(out_ref)

    slab = slab_ref[...]
    bins = slab.shape[0]
    for part, left_ref in enumerate(left_refs):
        left = left_ref[0]
        for b in range(left.shape[0]):
            kr_ref[pl.ds(b * bins, bins), :] = (left[b : b + 1, :] * slab).astype(kr_ref.dtype)
        prod = jnp.dot(x_ref[part], kr_ref[...], preferred_element_type=jnp.float32)
        row = rows_ref[GROUP * step + part]
        out_ref[row] = out_ref[row] + prod


def left_spec(shape, part):
    return pl.BlockSpec(shape, lambda i, rows, pl_: (pl_[GROUP * i + part], 0, 0))


def block_products(slab_blocks, received, places, block_row, factor_slab, row_blocks):
    count, edge, depth_k = slab_blocks.shape
    width = received.shape[2]
    grid_spec = pltpu.PrefetchScalarGridSpec(
        num_scalar_prefetch=2,
        grid=(count // GROUP,),
        in_specs=[pl.BlockSpec((GROUP, edge, depth_k), lambda i, rows, pl_: (i, 0, 0))]
        + [left_spec((1, received.shape[1], width), part) for part in range(GROUP)]
        + [pl.BlockSpec(factor_slab.shape, lambda i, rows, pl_: (0, 0))],
        out_specs=pl.BlockSpec((row_blocks, edge, width), lambda i, rows, pl_: (0, 0, 0)),
        scratch_shapes=[pltpu.VMEM((depth_k, width), jnp.bfloat16)],
    )
    flops = 2 * count * edge * depth_k * width
    return pl.pallas_call(
        mttkrp_kernel,
        grid_spec=grid_spec,
        out_shape=jax.ShapeDtypeStruct((row_blocks, edge, width), jnp.float32),
        compiler_params=pltpu.CompilerParams(
            dimension_semantics=("arbitrary",), vmem_limit_bytes=48 * 1024 * 1024
        ),
        cost_estimate=pl.CostEstimate(
            flops=flops,
            bytes_accessed=slab_blocks.size * 2 + count * edge * width * 2 + row_blocks * edge * width * 4,
            transcendentals=0,
        ),
    )(block_row, places, slab_blocks, *([received] * GROUP), factor_slab)


def scatter_sum(rows, peers):
    pieces = rows.reshape(peers, rows.shape[0] // peers, rows.shape[1])
    arrived = lax.all_to_all(pieces, "dst", split_axis=0, concat_axis=0, tiled=True)
    return jnp.sum(arrived, axis=0)


def exchange(pieces, peers):
    me = lax.axis_index("dst")
    got = [pieces[me][None]]
    for shift in range(1, peers):
        outgoing = lax.dynamic_index_in_dim(pieces, (me + shift) % peers, axis=0, keepdims=True)
        pairs = [(i, (i + shift) % peers) for i in range(peers)]
        got.append(lax.ppermute(outgoing, "dst", perm=pairs))
    by_shift = jnp.concatenate(got, axis=0)
    return jnp.take(by_shift, (me - jnp.arange(peers)) % peers, axis=0)


def ridge_inverse(gram):
    eye = jnp.eye(gram.shape[0], dtype=jnp.float32)
    start = eye / jnp.max(jnp.sum(jnp.abs(gram), axis=1))

    def going(state):
        steps, _, norm = state
        return (norm >= 1e-3) & (steps < 64)

    def step(state):
        steps, inverse, _ = state
        residual = eye - jnp.dot(gram, inverse, precision=lax.Precision.HIGHEST)
        norm = jnp.max(jnp.sum(jnp.abs(residual), axis=1))
        inverse = inverse + jnp.dot(inverse, residual, precision=lax.Precision.HIGHEST)
        return steps + 1, inverse, norm

    inverse = start
    for _ in range(9):
        level = lax.Precision.HIGH
        inverse = inverse + jnp.dot(inverse, eye - jnp.dot(gram, inverse, precision=level), precision=level)
    _, inverse, _ = lax.while_loop(going, step, (jnp.int32(0), inverse, jnp.float32(2.0)))
    return inverse


def shards(slab_blocks, owner_column, block_row, block_col, factor_dst, factor_slab, factor_old):
    peers = lax.axis_size("dst")
    count = slab_blocks.shape[0]
    edge = slab_blocks.shape[1]
    width = factor_dst.shape[1]
    depth = max(2, 4 * count // peers)
    owners = owner_column[:, 0]
    order = jnp.arange(count, dtype=jnp.int32)
    same = (owners[:, None] == owners[None, :]) & (order[None, :] < order[:, None])
    places = owners * depth + jnp.sum(same.astype(jnp.int32), axis=1)
    slot_ids = jnp.arange(peers * depth, dtype=jnp.int32)
    match = places[None, :] == slot_ids[:, None]
    requests = jnp.sum(jnp.where(match, block_col[None, :], 0), axis=1).reshape(peers, depth)
    local_gram = jnp.dot(factor_dst.T, factor_dst, preferred_element_type=jnp.float32)
    chunk = local_gram.shape[0] // peers
    asked_row = jnp.zeros((peers, 1, width), jnp.float32).at[:, 0, :depth].set(requests.astype(jnp.float32))
    first = jnp.concatenate([local_gram.reshape(peers, chunk, width), asked_row], axis=1)
    first = exchange(first, peers)
    gram_rows = jnp.sum(first[:, :chunk, :], axis=0)
    asked = first[:, chunk, :depth].astype(jnp.int32)
    spread = jnp.broadcast_to(gram_rows[None], (peers, chunk, width))
    gram_left = lax.all_to_all(spread, "dst", split_axis=0, concat_axis=0, tiled=True)
    gram_left = gram_left.reshape(peers * chunk, width)
    tiles_dst = factor_dst.reshape(factor_dst.shape[0] // edge, edge, width)
    outgoing = tiles_dst[asked.reshape(peers * depth)].reshape(peers, depth, edge, width)
    received = lax.all_to_all(outgoing, "dst", split_axis=0, concat_axis=0, tiled=True)
    received = received.reshape(peers * depth, edge, width)

    row_blocks = factor_old.shape[0] * peers // edge
    partial_sum = block_products(slab_blocks, received, places, block_row, factor_slab, row_blocks)
    partial_sum = partial_sum.reshape(row_blocks * edge, width)
    partial_sum, gram_left = lax.optimization_barrier((partial_sum, gram_left))
    summed_rows = scatter_sum(partial_sum, peers)

    gram_right = jnp.dot(factor_slab.T, factor_slab, preferred_element_type=jnp.float32)
    gram = gram_left * gram_right + RIDGE * jnp.eye(width, dtype=jnp.float32)
    inverse = ridge_inverse(gram)
    target = summed_rows + RIDGE * factor_old
    return jnp.dot(target, inverse, precision=lax.Precision.HIGHEST)


def solution(mesh):
    placed = (
        P(("src", "dst"), None, None),
        P(("src", "dst"), None),
        P(("src", "dst")),
        P(("src", "dst")),
        P("dst", None),
        P(),
        P(("src", "dst"), None),
    )
    return jax.shard_map(
        shards, mesh=mesh, in_specs=placed, out_specs=P(("src", "dst"), None), check_vma=False
    )
```
